32 devices in a mesh: snp: 8 (over z, y), samp: 4 (over x, core).
Axes of the slice: x: 2, y: 2, z: 4, core: 2. Of those that a mesh axis runs over, the one named last changes fastest.
Arguments:
- dosages: float32 [7168, 8192], P('snp', 'samp'), may hold values from 0 to 2, as said below
Outputs:
- linkage: float32 [7168, 3584], P('snp', 'samp')
The draws below stay inside these ranges and needn't reach their ends.
Inputs may be any that keep to these rules, and one draw needn't show every extreme that they name: `dosages`: continuous imputed dosage of a SNP in a sample.
All inputs are finite; a program needn't handle non-finite values.
Results may differ from the reference program's by a relative error of at most 0.00096.
Values may be sent and summed in bfloat16 or wider, within the bound.
No kernel may reach another device: no remote copies, remote signals or barrier semaphores. Data moves between devices by JAX's collectives and lax.ppermute only.
A program may use at most 128 MiB of HBM per device.

```python
import jax
import jax.numpy as jnp
from jax import lax

SNP_DEV = 896
BAND = 3
SNPS = 7168
SAMPLES = 8192
N_SNP = 8


def draw_dosages(key, part):
    seg_len = max(SNP_DEV // 8, 1)
    seg_total = SNPS // seg_len + BAND * 8
    key_bits, key_freq, key_mix, key_offset, key_shared, key_noise, key_spread = jax.random.split(key, 7)
    raw_bits = jax.random.randint(key_bits, (SNPS, SAMPLES), 0, 2 ** 30)
    allele_freq = jax.random.randint(key_freq, (SNPS, 1), 100, 501)
    mix_rate = jax.random.randint(key_mix, (SNPS, 1), 0, 91)
    seg_offset = jax.random.randint(key_offset, (SNPS,), 0, BAND * 8)
    shared_geno = jax.random.randint(key_shared, (seg_total, SAMPLES), 0, 3)
    seg_index = jnp.arange(SNPS, dtype=jnp.int32) // seg_len + seg_offset
    chosen_geno = jnp.take(shared_geno, seg_index, axis=0)
    first_draw = raw_bits % 1000
    second_draw = raw_bits // 1000 % 1000
    own_geno = (first_draw < allele_freq).astype(jnp.int32) + (second_draw < allele_freq).astype(jnp.int32)
    pick_mask = raw_bits // 1000000 % 100 < mix_rate
    genotype = jnp.where(pick_mask, chosen_geno, own_geno)
    spread = jax.random.uniform(key_spread, (SNPS, 1), jnp.float32, 0.1, 0.3)
    unit = jax.random.uniform(key_noise, (SNPS, SAMPLES), jnp.float32)
    low_value = unit * spread
    high_value = 2.0 - unit * spread
    middle_value = 1.0 + (2.0 * unit - 1.0) * spread
    dosage = jnp.where(genotype == 0, low_value, jnp.where(genotype == 2, high_value, middle_value))
    return dosage.astype(jnp.float32)


def setup_inputs(seed: int = 0) -> dict:
    keys = jax.random.split(jax.random.key(seed), 2)
    return {
        "dosages": draw_dosages(jax.random.fold_in(keys[1], 71), 0),
    }


def reference(dosages):
    values = dosages.astype(jnp.float32)
    mean = lax.optimization_barrier(jnp.sum(values, axis=1)) / SAMPLES
    variance = lax.optimization_barrier(jnp.sum(values * values, axis=1)) / SAMPLES - mean * mean
    standard = ((values - mean[:, None]) * lax.rsqrt(variance + 1e-05)[:, None]).astype(jnp.bfloat16)
    padded = jnp.concatenate([standard, jnp.zeros((BAND * SNP_DEV, SAMPLES), jnp.bfloat16)], axis=0)

    def one_block(block_index):
        start = (block_index * SNP_DEV).astype(jnp.int32)
        own_rows = lax.dynamic_slice_in_dim(padded, start, SNP_DEV, 0).astype(jnp.float32)
        window = lax.dynamic_slice_in_dim(padded, start, (BAND + 1) * SNP_DEV, 0).astype(jnp.float32)
        gram = lax.dot_general(own_rows, window, (((1,), (1,)), ((), ())), precision=lax.Precision.HIGHEST, preferred_element_type=jnp.float32)
        return gram / SAMPLES
    tiles = lax.map(one_block, jnp.arange(N_SNP, dtype=jnp.int32))
    return tiles.reshape(SNPS, (BAND + 1) * SNP_DEV)
```

```python
import jax
import jax.numpy as jnp
from jax import lax
from jax.sharding import PartitionSpec as P

BAND = 3
CHUNKS = 8


def moved(value, pairs):
    return lax.ppermute(value, "snp", pairs)


def standardize(values, sums, squares, total):
    mean = sums / total
    variance = squares / total - mean * mean
    return ((values - mean[:, None]) * lax.rsqrt(variance + 1e-05)[:, None]).astype(jnp.bfloat16)


def local_moments(values):
    return (jnp.sum(values, axis=1), jnp.sum(values * values, axis=1))


def local(dosages):
    total = dosages.shape[1] * lax.axis_size("samp")
    count = lax.axis_size("snp")
    sums, squares = local_moments(dosages)
    sums, squares = lax.psum((sums, squares), "samp")
    own_block = standardize(dosages, sums, squares, total)
    rows = own_block.shape[0]
    step = rows // CHUNKS
    pieces = [own_block[c * step:(c + 1) * step] for c in range(CHUNKS)]

    odd = list(range(1, count, 2))
    even = list(range(0, count, 2))
    z_down = [(s, s - 2) for s in range(2, count)]
    odd_to_even = [(s, s - 1) for s in odd]
    even_to_odd = [(s, s + 1) for s in even if s + 1 < count]
    odd_down = [(s, s - 2) for s in odd if s >= 3]

    two = [None] * CHUNKS
    one_even = [None] * CHUNKS
    one_odd = [None] * CHUNKS
    three_even = [None] * CHUNKS
    three_odd = [None] * CHUNKS
    results = [None] * CHUNKS

    def finish(c):
        blocks = [pieces[c], one_even[c] + one_odd[c], two[c], three_even[c] + three_odd[c]]
        tiles = [
            jnp.einsum("ab,cb->ac", own_block, other, preferred_element_type=jnp.float32)
            for other in blocks
        ]
        partial_gram = jnp.concatenate(tiles, axis=1)
        results[c] = lax.psum_scatter(partial_gram, "samp", scatter_dimension=1, tiled=True)

    for t in range(CHUNKS + 2):
        if t < CHUNKS:
            two[t] = moved(pieces[t], z_down)
            one_even[t] = moved(pieces[t], odd_to_even)
        if 0 <= t - 1 < CHUNKS:
            c = t - 1
            one_odd[c] = moved(two[c], even_to_odd)
            three_even[c] = moved(two[c], odd_to_even)
        if 0 <= t - 2 < CHUNKS:
            c = t - 2
            three_odd[c] = moved(one_odd[c], odd_down)
        if 0 <= t - 3 < CHUNKS:
            finish(t - 3)
        carried = (two, one_even, one_odd, three_even, three_odd)
        flat, tree = jax.tree.flatten(carried)
        following = pieces[t + 1] if t + 1 < CHUNKS else own_block[:8]
        flat, following = lax.optimization_barrier((flat, following))
        two, one_even, one_odd, three_even, three_odd = [list(x) for x in jax.tree.unflatten(tree, flat)]
        if t + 1 < CHUNKS:
            pieces[t + 1] = following
    for c in range(CHUNKS):
        if results[c] is None:
            finish(c)
    summed = jnp.concatenate(results, axis=1)
    return summed / total


def solution(mesh):
    return jax.shard_map(
        local,
        mesh=mesh,
        in_specs=(P("snp", "samp"),),
        out_specs=P("snp", "samp"),
        check_vma=False,
    )
```

```python
import jax
import jax.numpy as jnp
from jax import lax
from jax.sharding import PartitionSpec as P

BAND = 3
CHUNKS = 8


def moved(value, pairs):
    return lax.ppermute(value, "snp", pairs)


def standardize(values, sums, squares, total):
    mean = sums / total
    variance = squares / total - mean * mean
    return ((values - mean[:, None]) * lax.rsqrt(variance + 1e-05)[:, None]).astype(jnp.bfloat16)


def local_moments(values):
    return (jnp.sum(values, axis=1), jnp.sum(values * values, axis=1))


def joined(parts):
    parts = [p for p in parts if p is not None]
    return parts[0] if len(parts) == 1 else jnp.concatenate(parts, axis=0)


def local(dosages):
    total = dosages.shape[1] * lax.axis_size("samp")
    count = lax.axis_size("snp")
    groups = lax.axis_size("samp")
    sums, squares = local_moments(dosages)
    sums, squares = lax.psum((sums, squares), "samp")
    own_block = standardize(dosages, sums, squares, total)
    rows = own_block.shape[0]
    step = rows // CHUNKS
    pieces = [own_block[c * step:(c + 1) * step] for c in range(CHUNKS)]

    odd = list(range(1, count, 2))
    even = list(range(0, count, 2))
    z_down = [(s, s - 2) for s in range(2, count)]
    odd_to_even = [(s, s - 1) for s in odd]
    even_to_odd = [(s, s + 1) for s in even if s + 1 < count]

    me = lax.axis_index("samp")
    order = jnp.bitwise_xor(me, jnp.arange(BAND + 1, dtype=me.dtype))
    partner = [(j, j ^ 1) for j in range(groups)]
    across = [(j, j ^ 2) for j in range(groups)]

    names = ("two", "one_even", "one_odd", "three_even", "three_odd", "tiles", "first", "results")
    state = {name: [None] * CHUNKS for name in names}

    def finish(c):
        blocks = jnp.stack([
            pieces[c],
            state["one_even"][c] + state["one_odd"][c],
            state["two"][c],
            state["three_even"][c] + state["three_odd"][c],
        ])
        picked = jnp.take(blocks, order, axis=0).reshape((BAND + 1) * step, -1)
        state["tiles"][c] = jnp.einsum("ab,cb->ac", own_block, picked, preferred_element_type=jnp.float32)

    def tile(c, k):
        return state["tiles"][c][:, k * step:(k + 1) * step]

    for t in range(CHUNKS + 4):
        new = t if t < CHUNKS else None
        second = t - 1 if 0 <= t - 1 < CHUNKS else None
        third = t - 2 if 0 <= t - 2 < CHUNKS else None
        if new is not None or third is not None:
            sent = moved(joined([pieces[new] if new is not None else None,
                                 state["one_odd"][third] if third is not None else None]), z_down)
            if new is not None:
                state["two"][new] = sent[:step]
            if third is not None:
                state["three_odd"][third] = sent[-step:]
        if new is not None or second is not None:
            sent = moved(joined([pieces[new] if new is not None else None,
                                 state["two"][second] if second is not None else None]), odd_to_even)
            if new is not None:
                state["one_even"][new] = sent[:step]
            if second is not None:
                state["three_even"][second] = sent[-step:]
        if second is not None:
            state["one_odd"][second] = moved(state["two"][second], even_to_odd)
        if 0 <= t - 3 < CHUNKS:
            c = t - 3
            finish(c)
            payload = jnp.concatenate([tile(c, 1), tile(c, 3)], axis=1)
            state["first"][c] = lax.ppermute(payload, "samp", partner)
        if 0 <= t - 4 < CHUNKS:
            c = t - 4
            payload = tile(c, 2) + state["first"][c][:, step:]
            last = lax.ppermute(payload, "samp", across)
            state["results"][c] = tile(c, 0) + state["first"][c][:, :step] + last
        flat, tree = jax.tree.flatten(state)
        following = pieces[t + 1] if t + 1 < CHUNKS else own_block[:8]
        flat, following = lax.optimization_barrier((flat, following))
        state = {k: list(v) for k, v in jax.tree.unflatten(tree, flat).items()}
        if t + 1 < CHUNKS:
            pieces[t + 1] = following
    summed = jnp.concatenate(state["results"], axis=1)
    return summed / total


def solution(mesh):
    return jax.shard_map(
        local,
        mesh=mesh,
        in_specs=(P("snp", "samp"),),
        out_specs=P("snp", "samp"),
        check_vma=False,
    )
```

```python
import jax
import jax.numpy as jnp
from jax import lax
from jax.sharding import PartitionSpec as P

BAND = 3
CHUNKS = 8


def moved(value, pairs):
    return lax.ppermute(value, "snp", pairs)


def standardize(values, sums, squares, total):
    mean = sums / total
    variance = squares / total - mean * mean
    return ((values - mean[:, None]) * lax.rsqrt(variance + 1e-05)[:, None]).astype(jnp.bfloat16)


def local_moments(values):
    return (jnp.sum(values, axis=1), jnp.sum(values * values, axis=1))


def joined(parts):
    parts = [p for p in parts if p is not None]
    return parts[0] if len(parts) == 1 else jnp.concatenate(parts, axis=0)


def local(dosages):
    total = dosages.shape[1] * lax.axis_size("samp")
    count = lax.axis_size("snp")
    groups = lax.axis_size("samp")
    sums, squares = local_moments(dosages)
    sums, squares = lax.psum((sums, squares), "samp")
    own_block = standardize(dosages, sums, squares, total)
    rows = own_block.shape[0]
    step = rows // CHUNKS
    pieces = [own_block[c * step:(c + 1) * step] for c in range(CHUNKS)]

    odd = list(range(1, count, 2))
    even = list(range(0, count, 2))
    z_down = [(s, s - 2) for s in range(2, count)]
    odd_to_even = [(s, s - 1) for s in odd]
    even_to_odd = [(s, s + 1) for s in even if s + 1 < count]

    me = lax.axis_index("samp")
    even_me = me % 2 == 0
    low = me < 2
    partner = [(j, j ^ 1) for j in range(groups)]
    across = [(j, j ^ 2) for j in range(groups)]

    names = ("two", "one_even", "one_odd", "three_even", "three_odd", "tiles", "first", "results")
    state = {name: [None] * CHUNKS for name in names}

    def finish(c):
        blocks = [
            pieces[c],
            state["one_even"][c] + state["one_odd"][c],
            state["two"][c],
            state["three_even"][c] + state["three_odd"][c],
        ]
        state["tiles"][c] = [
            jnp.einsum("ab,cb->ac", own_block, other, preferred_element_type=jnp.float32)
            for other in blocks
        ]

    def pick(c, a, b, d, e):
        t = state["tiles"][c]
        return jnp.where(low, jnp.where(even_me, t[a], t[b]), jnp.where(even_me, t[d], t[e]))

    for t in range(CHUNKS + 4):
        new = t if t < CHUNKS else None
        second = t - 1 if 0 <= t - 1 < CHUNKS else None
        third = t - 2 if 0 <= t - 2 < CHUNKS else None
        if new is not None or third is not None:
            sent = moved(joined([pieces[new] if new is not None else None,
                                 state["one_odd"][third] if third is not None else None]), z_down)
            if new is not None:
                state["two"][new] = sent[:step]
            if third is not None:
                state["three_odd"][third] = sent[-step:]
        if new is not None or second is not None:
            sent = moved(joined([pieces[new] if new is not None else None,
                                 state["two"][second] if second is not None else None]), odd_to_even)
            if new is not None:
                state["one_even"][new] = sent[:step]
            if second is not None:
                state["three_even"][second] = sent[-step:]
        if second is not None:
            state["one_odd"][second] = moved(state["two"][second], even_to_odd)
        if 0 <= t - 3 < CHUNKS:
            c = t - 3
            finish(c)
            tiles = state["tiles"][c]
            payload = jnp.where(even_me, jnp.concatenate([tiles[1], tiles[3]], axis=1),
                                jnp.concatenate([tiles[0], tiles[2]], axis=1))
            state["first"][c] = lax.ppermute(payload, "samp", partner)
        if 0 <= t - 4 < CHUNKS:
            c = t - 4
            got = state["first"][c]
            mine = jnp.where(low, got[:, :step], got[:, step:])
            onward = jnp.where(low, got[:, step:], got[:, :step])
            last = lax.ppermute(pick(c, 2, 3, 0, 1) + onward, "samp", across)
            state["results"][c] = pick(c, 0, 1, 2, 3) + mine + last
        flat, tree = jax.tree.flatten(state)
        following = pieces[t + 1] if t + 1 < CHUNKS else own_block[:8]
        flat, following = lax.optimization_barrier((flat, following))
        state = {k: list(v) for k, v in jax.tree.unflatten(tree, flat).items()}
        if t + 1 < CHUNKS:
            pieces[t + 1] = following
    summed = jnp.concatenate(state["results"], axis=1)
    return summed / total


def solution(mesh):
    return jax.shard_map(
        local,
        mesh=mesh,
        in_specs=(P("snp", "samp"),),
        out_specs=P("snp", "samp"),
        check_vma=False,
    )
```

```python
import jax
import jax.numpy as jnp
from jax import lax
from jax.sharding import PartitionSpec as P

BAND = 3
CHUNKS = 8


def moved(value, pairs):
    return lax.ppermute(value, "snp", pairs)


def standardize(values, sums, squares, total):
    mean = sums / total
    variance = squares / total - mean * mean
    return ((values - mean[:, None]) * lax.rsqrt(variance + 1e-05)[:, None]).astype(jnp.bfloat16)


def local_moments(values):
    return (jnp.sum(values, axis=1), jnp.sum(values * values, axis=1))


def joined(parts):
    parts = [p for p in parts if p is not None]
    return parts[0] if len(parts) == 1 else jnp.concatenate(parts, axis=0)


def local(dosages):
    total = dosages.shape[1] * lax.axis_size("samp")
    count = lax.axis_size("snp")
    groups = lax.axis_size("samp")
    sums, squares = local_moments(dosages)
    sums, squares = lax.psum((sums, squares), "samp")
    own_block = standardize(dosages, sums, squares, total)
    rows = own_block.shape[0]
    step = rows // CHUNKS
    pieces = [own_block[c * step:(c + 1) * step] for c in range(CHUNKS)]

    odd = list(range(1, count, 2))
    even = list(range(0, count, 2))
    z_down = [(s, s - 2) for s in range(2, count)]
    odd_to_even = [(s, s - 1) for s in odd]
    even_to_odd = [(s, s + 1) for s in even if s + 1 < count]
    even_to_odd_below = [(s, s - 1) for s in even if s >= 2]

    me = lax.axis_index("samp")
    even_me = me % 2 == 0
    low = me < 2
    partner = [(j, j ^ 1) for j in range(groups)]
    across = [(j, j ^ 2) for j in range(groups)]

    names = ("two", "one_even", "one_odd", "three_even", "three_odd", "tiles", "first", "results")
    state = {name: [None] * CHUNKS for name in names}

    def finish(c):
        blocks = [
            pieces[c],
            state["one_even"][c] + state["one_odd"][c],
            state["two"][c],
            state["three_even"][c] + state["three_odd"][c],
        ]
        state["tiles"][c] = [
            jnp.einsum("ab,cb->ac", own_block, other, preferred_element_type=jnp.float32)
            for other in blocks
        ]

    def pick(c, a, b, d, e):
        t = state["tiles"][c]
        return jnp.where(low, jnp.where(even_me, t[a], t[b]), jnp.where(even_me, t[d], t[e]))

    for t in range(CHUNKS + 4):
        new = t if t < CHUNKS else None
        second = t - 1 if 0 <= t - 1 < CHUNKS else None
        third = t - 2 if 0 <= t - 2 < CHUNKS - 1 else None
        if new is not None or third is not None:
            sent = moved(joined([pieces[new] if new is not None else None,
                                 state["one_odd"][third] if third is not None else None]), z_down)
            if new is not None:
                state["two"][new] = sent[:step]
            if third is not None:
                state["three_odd"][third] = sent[-step:]
        if new is not None or second is not None:
            sent = moved(joined([pieces[new] if new is not None else None,
                                 state["two"][second] if second is not None else None]), odd_to_even)
            if new is not None:
                state["one_even"][new] = sent[:step]
            if second is not None:
                state["three_even"][second] = sent[-step:]
        if second is not None:
            state["one_odd"][second] = moved(state["two"][second], even_to_odd)
            if second == CHUNKS - 1:
                state["three_odd"][second] = moved(state["two"][second], even_to_odd_below)
        if 0 <= t - 3 < CHUNKS:
            c = t - 3
            finish(c)
            tiles = state["tiles"][c]
            payload = jnp.where(even_me, jnp.concatenate([tiles[1], tiles[3]], axis=1),
                                jnp.concatenate([tiles[0], tiles[2]], axis=1))
            state["first"][c] = lax.ppermute(payload, "samp", partner)
        if 0 <= t - 4 < CHUNKS:
            c = t - 4
            got = state["first"][c]
            mine = jnp.where(low, got[:, :step], got[:, step:])
            onward = jnp.where(low, got[:, step:], got[:, :step])
            last = lax.ppermute(pick(c, 2, 3, 0, 1) + onward, "samp", across)
            state["results"][c] = pick(c, 0, 1, 2, 3) + mine + last
        if t + 1 < CHUNKS:
            flat, tree = jax.tree.flatten(state)
            flat, pieces[t + 1] = lax.optimization_barrier((flat, pieces[t + 1]))
            state = {k: list(v) for k, v in jax.tree.unflatten(tree, flat).items()}
    summed = jnp.concatenate(state["results"], axis=1)
    return summed / total


def solution(mesh):
    return jax.shard_map(
        local,
        mesh=mesh,
        in_specs=(P("snp", "samp"),),
        out_specs=P("snp", "samp"),
        check_vma=False,
    )
```

```python
import jax
import jax.numpy as jnp
from jax import lax
from jax.sharding import PartitionSpec as P

BAND = 3
CHUNKS = 8


def moved(value, pairs):
    return lax.ppermute(value, "snp", pairs)


def standardize(values, sums, squares, total):
    mean = sums / total
    variance = squares / total - mean * mean
    return ((values - mean[:, None]) * lax.rsqrt(variance + 1e-05)[:, None]).astype(jnp.bfloat16)


def local_moments(values):
    return (jnp.sum(values, axis=1), jnp.sum(values * values, axis=1))


def joined(parts):
    parts = [p for p in parts if p is not None]
    return parts[0] if len(parts) == 1 else jnp.concatenate(parts, axis=0)


def local(dosages):
    total = dosages.shape[1] * lax.axis_size("samp")
    count = lax.axis_size("snp")
    groups = lax.axis_size("samp")
    sums, squares = local_moments(dosages)
    sums, squares = lax.psum((sums, squares), "samp")
    own_block = standardize(dosages, sums, squares, total)
    rows = own_block.shape[0]
    step = rows // CHUNKS
    pieces = [own_block[c * step:(c + 1) * step] for c in range(CHUNKS)]

    odd = list(range(1, count, 2))
    even = list(range(0, count, 2))
    z_down = [(s, s - 2) for s in range(2, count)]
    odd_to_even = [(s, s - 1) for s in odd]
    even_to_odd = [(s, s + 1) for s in even if s + 1 < count]
    even_to_odd_below = [(s, s - 1) for s in even if s >= 2]

    me = lax.axis_index("samp")
    even_me = me % 2 == 0
    low = me < 2
    partner = [(j, j ^ 1) for j in range(groups)]
    across = [(j, j ^ 2) for j in range(groups)]

    names = ("two", "one_even", "one_odd", "three_even", "three_odd", "tiles", "first", "results")
    state = {name: [None] * CHUNKS for name in names}

    def finish(c):
        blocks = [
            pieces[c],
            state["one_even"][c] + state["one_odd"][c],
            state["two"][c],
            state["three_even"][c] + state["three_odd"][c],
        ]
        state["tiles"][c] = [
            jnp.einsum("ab,cb->ac", own_block, other, preferred_element_type=jnp.float32)
            for other in blocks
        ]

    def pick(c, a, b, d, e):
        t = state["tiles"][c]
        return jnp.where(low, jnp.where(even_me, t[a], t[b]), jnp.where(even_me, t[d], t[e]))

    ready = [c + 3 for c in range(CHUNKS - 1)] + [CHUNKS + 1]
    for t in range(CHUNKS + 3):
        new = t if t < CHUNKS else None
        second = t - 1 if 0 <= t - 1 < CHUNKS else None
        third = t - 2 if 0 <= t - 2 < CHUNKS - 1 else None
        if new is not None or third is not None:
            sent = moved(joined([pieces[new] if new is not None else None,
                                 state["one_odd"][third] if third is not None else None]), z_down)
            if new is not None:
                state["two"][new] = sent[:step]
            if third is not None:
                state["three_odd"][third] = sent[-step:]
        if new is not None or second is not None:
            sent = moved(joined([pieces[new] if new is not None else None,
                                 state["two"][second] if second is not None else None]), odd_to_even)
            if new is not None:
                state["one_even"][new] = sent[:step]
            if second is not None:
                state["three_even"][second] = sent[-step:]
        if second is not None:
            state["one_odd"][second] = moved(state["two"][second], even_to_odd)
            if second == CHUNKS - 1:
                state["three_odd"][second] = moved(state["two"][second], even_to_odd_below)
        for c in [c for c in range(CHUNKS) if ready[c] == t]:
            finish(c)
            tiles = state["tiles"][c]
            payload = jnp.where(even_me, jnp.concatenate([tiles[1], tiles[3]], axis=1),
                                jnp.concatenate([tiles[0], tiles[2]], axis=1))
            state["first"][c] = lax.ppermute(payload, "samp", partner)
        for c in [c for c in range(CHUNKS) if ready[c] + 1 == t]:
            got = state["first"][c]
            mine = jnp.where(low, got[:, :step], got[:, step:])
            onward = jnp.where(low, got[:, step:], got[:, :step])
            last = lax.ppermute(pick(c, 2, 3, 0, 1) + onward, "samp", across)
            state["results"][c] = pick(c, 0, 1, 2, 3) + mine + last
        flat, tree = jax.tree.flatten(state)
        following = pieces[t + 1] if t + 1 < CHUNKS else own_block[:8]
        flat, following = lax.optimization_barrier((flat, following))
        state = {k: list(v) for k, v in jax.tree.unflatten(tree, flat).items()}
        if t + 1 < CHUNKS:
            pieces[t + 1] = following
    summed = jnp.concatenate(state["results"], axis=1)
    return summed / total


def solution(mesh):
    return jax.shard_map(
        local,
        mesh=mesh,
        in_specs=(P("snp", "samp"),),
        out_specs=P("snp", "samp"),
        check_vma=False,
    )
```

```python
import jax
import jax.numpy as jnp
from jax import lax
from jax.sharding import PartitionSpec as P

BAND = 3
CHUNKS = 8


def moved(value, pairs):
    return lax.ppermute(value, "snp", pairs)


def standardize(values, sums, squares, total):
    mean = sums / total
    variance = squares / total - mean * mean
    return ((values - mean[:, None]) * lax.rsqrt(variance + 1e-05)[:, None]).astype(jnp.bfloat16)


def local_moments(values):
    return (jnp.sum(values, axis=1), jnp.sum(values * values, axis=1))


def joined(parts):
    parts = [p for p in parts if p is not None]
    return parts[0] if len(parts) == 1 else jnp.concatenate(parts, axis=0)


def local(dosages):
    total = dosages.shape[1] * lax.axis_size("samp")
    count = lax.axis_size("snp")
    groups = lax.axis_size("samp")
    me = lax.axis_index("samp")
    flips = list(range(1, groups))

    def choose(values):
        ordered = []
        for k in range(groups):
            pick = values[0]
            for i in flips:
                pick = jnp.where(jnp.bitwise_xor(me, i) == k, values[i], pick)
            ordered.append(pick)
        return ordered

    def added(values):
        ordered = choose(values)
        result = ordered[0]
        for part in ordered[1:]:
            result = result + part
        return result

    moments = jnp.stack(local_moments(dosages))
    summed_moments = added(
        [moments] + [lax.ppermute(moments, "samp", [(j, j ^ i) for j in range(groups)]) for i in flips])
    own_block = standardize(dosages, summed_moments[0], summed_moments[1], total)
    rows = own_block.shape[0]
    step = rows // CHUNKS
    pieces = [own_block[c * step:(c + 1) * step] for c in range(CHUNKS)]

    odd = list(range(1, count, 2))
    even = list(range(0, count, 2))
    z_down = [(s, s - 2) for s in range(2, count)]
    odd_to_even = [(s, s - 1) for s in odd]
    even_to_odd = [(s, s + 1) for s in even if s + 1 < count]

    names = ("two", "one_even", "one_odd", "three_even", "three_odd", "results")
    state = {name: [None] * CHUNKS for name in names}

    def finish(c):
        blocks = jnp.concatenate([
            pieces[c],
            state["one_even"][c] + state["one_odd"][c],
            state["two"][c],
            state["three_even"][c] + state["three_odd"][c],
        ], axis=0)
        gram = jnp.einsum("ab,cb->ac", own_block, blocks, preferred_element_type=jnp.float32)
        tiles = [gram[:, k * step:(k + 1) * step] for k in range(BAND + 1)]
        outgoing = []
        for i in [0] + flips:
            target = tiles[0]
            for k in range(1, groups):
                target = jnp.where(jnp.bitwise_xor(me, i) == k, tiles[k], target)
            outgoing.append(target)
        arrived = [outgoing[0]] + [
            lax.ppermute(outgoing[i], "samp", [(j, j ^ i) for j in range(groups)]) for i in flips]
        state["results"][c] = added(arrived)

    for t in range(CHUNKS + 3):
        new = t if t < CHUNKS else None
        second = t - 1 if 0 <= t - 1 < CHUNKS else None
        third = t - 2 if 0 <= t - 2 < CHUNKS else None
        if new is not None or third is not None:
            sent = moved(joined([pieces[new] if new is not None else None,
                                 state["one_odd"][third] if third is not None else None]), z_down)
            if new is not None:
                state["two"][new] = sent[:step]
            if third is not None:
                state["three_odd"][third] = sent[-step:]
        if new is not None or second is not None:
            sent = moved(joined([pieces[new] if new is not None else None,
                                 state["two"][second] if second is not None else None]), odd_to_even)
            if new is not None:
                state["one_even"][new] = sent[:step]
            if second is not None:
                state["three_even"][second] = sent[-step:]
        if second is not None:
            state["one_odd"][second] = moved(state["two"][second], even_to_odd)
        if 0 <= t - 3 < CHUNKS:
            finish(t - 3)
        flat, tree = jax.tree.flatten(state)
        following = pieces[t + 1] if t + 1 < CHUNKS else own_block[:8]
        flat, following = lax.optimization_barrier((flat, following))
        state = {k: list(v) for k, v in jax.tree.unflatten(tree, flat).items()}
        if t + 1 < CHUNKS:
            pieces[t + 1] = following
    summed = jnp.concatenate(state["results"], axis=1)
    return summed / total


def solution(mesh):
    return jax.shard_map(
        local,
        mesh=mesh,
        in_specs=(P("snp", "samp"),),
        out_specs=P("snp", "samp"),
        check_vma=False,
    )
```

```python
import jax
import jax.numpy as jnp
from jax import lax
from jax.sharding import PartitionSpec as P

BAND = 3
CHUNKS = 8


def moved(value, pairs):
    return lax.ppermute(value, "snp", pairs)


def standardize(values, sums, squares, total):
    mean = sums / total
    variance = squares / total - mean * mean
    return ((values - mean[:, None]) * lax.rsqrt(variance + 1e-05)[:, None]).astype(jnp.bfloat16)


def local_moments(values):
    return (jnp.sum(values, axis=1), jnp.sum(values * values, axis=1))


def joined(parts):
    parts = [p for p in parts if p is not None]
    return parts[0] if len(parts) == 1 else jnp.concatenate(parts, axis=0)


def local(dosages):
    total = dosages.shape[1] * lax.axis_size("samp")
    count = lax.axis_size("snp")
    groups = lax.axis_size("samp")
    me = lax.axis_index("samp")
    flips = list(range(1, groups))

    def choose(values):
        ordered = []
        for k in range(groups):
            pick = values[0]
            for i in flips:
                pick = jnp.where(jnp.bitwise_xor(me, i) == k, values[i], pick)
            ordered.append(pick)
        return ordered

    def added(values):
        ordered = choose(values)
        result = ordered[0]
        for part in ordered[1:]:
            result = result + part
        return result

    moments = jnp.stack(local_moments(dosages))
    summed_moments = added(
        [moments] + [lax.ppermute(moments, "samp", [(j, j ^ i) for j in range(groups)]) for i in flips])
    own_block = standardize(dosages, summed_moments[0], summed_moments[1], total)
    rows = own_block.shape[0]
    step = rows // CHUNKS
    pieces = [own_block[c * step:(c + 1) * step] for c in range(CHUNKS)]

    odd = list(range(1, count, 2))
    even = list(range(0, count, 2))
    z_down = [(s, s - 2) for s in range(2, count)]
    odd_to_even = [(s, s - 1) for s in odd]
    even_to_odd = [(s, s + 1) for s in even if s + 1 < count]

    even_me = me % 2 == 0
    low = me < 2
    partner = [(j, j ^ 1) for j in range(groups)]
    across = [(j, j ^ 2) for j in range(groups)]

    names = ("two", "one_even", "one_odd", "three_even", "three_odd", "tiles", "first", "results")
    state = {name: [None] * CHUNKS for name in names}

    def finish(c):
        blocks = jnp.concatenate([
            pieces[c],
            state["one_even"][c] + state["one_odd"][c],
            state["two"][c],
            state["three_even"][c] + state["three_odd"][c],
        ], axis=0)
        gram = jnp.einsum("ab,cb->ac", own_block, blocks, preferred_element_type=jnp.float32)
        tiles = [gram[:, k * step:(k + 1) * step] for k in range(BAND + 1)]
        state["tiles"][c] = tiles
        if c == CHUNKS - 1:
            outgoing = []
            for i in [0] + flips:
                target = tiles[0]
                for k in range(1, groups):
                    target = jnp.where(jnp.bitwise_xor(me, i) == k, tiles[k], target)
                outgoing.append(target)
            arrived = [outgoing[0]] + [
                lax.ppermute(outgoing[i], "samp", [(j, j ^ i) for j in range(groups)]) for i in flips]
            state["results"][c] = added(arrived)
        else:
            payload = jnp.where(even_me, jnp.concatenate([tiles[1], tiles[3]], axis=1),
                                jnp.concatenate([tiles[0], tiles[2]], axis=1))
            state["first"][c] = lax.ppermute(payload, "samp", partner)

    def pick(c, a, b, d, e):
        t = state["tiles"][c]
        return jnp.where(low, jnp.where(even_me, t[a], t[b]), jnp.where(even_me, t[d], t[e]))

    def second_level(c):
        got = state["first"][c]
        mine = jnp.where(low, got[:, :step], got[:, step:])
        onward = jnp.where(low, got[:, step:], got[:, :step])
        last = lax.ppermute(pick(c, 2, 3, 0, 1) + onward, "samp", across)
        state["results"][c] = pick(c, 0, 1, 2, 3) + mine + last

    for t in range(CHUNKS + 3):
        new = t if t < CHUNKS else None
        second = t - 1 if 0 <= t - 1 < CHUNKS else None
        third = t - 2 if 0 <= t - 2 < CHUNKS else None
        if new is not None or third is not None:
            sent = moved(joined([pieces[new] if new is not None else None,
                                 state["one_odd"][third] if third is not None else None]), z_down)
            if new is not None:
                state["two"][new] = sent[:step]
            if third is not None:
                state["three_odd"][third] = sent[-step:]
        if new is not None or second is not None:
            sent = moved(joined([pieces[new] if new is not None else None,
                                 state["two"][second] if second is not None else None]), odd_to_even)
            if new is not None:
                state["one_even"][new] = sent[:step]
            if second is not None:
                state["three_even"][second] = sent[-step:]
        if second is not None:
            state["one_odd"][second] = moved(state["two"][second], even_to_odd)
        if 0 <= t - 3 < CHUNKS:
            finish(t - 3)
        if 0 <= t - 4 < CHUNKS - 1:
            second_level(t - 4)
        flat, tree = jax.tree.flatten(state)
        following = pieces[t + 1] if t + 1 < CHUNKS else own_block[:8]
        flat, following = lax.optimization_barrier((flat, following))
        state = {k: list(v) for k, v in jax.tree.unflatten(tree, flat).items()}
        if t + 1 < CHUNKS:
            pieces[t + 1] = following
    summed = jnp.concatenate(state["results"], axis=1)
    return summed / total


def solution(mesh):
    return jax.shard_map(
        local,
        mesh=mesh,
        in_specs=(P("snp", "samp"),),
        out_specs=P("snp", "samp"),
        check_vma=False,
    )
```

```python
import jax
import jax.numpy as jnp
from jax import lax
from jax.sharding import PartitionSpec as P

BAND = 3
CHUNKS = 8


def moved(value, pairs):
    return lax.ppermute(value, "snp", pairs)


def standardize(values, sums, squares, total):
    mean = sums / total
    variance = squares / total - mean * mean
    return ((values - mean[:, None]) * lax.rsqrt(variance + 1e-05)[:, None]).astype(jnp.bfloat16)


def local_moments(values):
    return (jnp.sum(values, axis=1), jnp.sum(values * values, axis=1))


def joined(parts):
    parts = [p for p in parts if p is not None]
    return parts[0] if len(parts) == 1 else jnp.concatenate(parts, axis=0)


def local(dosages):
    total = dosages.shape[1] * lax.axis_size("samp")
    count = lax.axis_size("snp")
    groups = lax.axis_size("samp")
    me = lax.axis_index("samp")
    flips = list(range(1, groups))

    def choose(values):
        ordered = []
        for k in range(groups):
            pick = values[0]
            for i in flips:
                pick = jnp.where(jnp.bitwise_xor(me, i) == k, values[i], pick)
            ordered.append(pick)
        return ordered

    def added(values):
        ordered = choose(values)
        result = ordered[0]
        for part in ordered[1:]:
            result = result + part
        return result

    moments = jnp.stack(local_moments(dosages))
    summed_moments = added(
        [moments] + [lax.ppermute(moments, "samp", [(j, j ^ i) for j in range(groups)]) for i in flips])
    own_block = standardize(dosages, summed_moments[0], summed_moments[1], total)
    rows = own_block.shape[0]
    edge = rows // (2 * CHUNKS - 2)
    sizes = [edge] + [2 * edge] * (CHUNKS - 2) + [rows - edge * (2 * CHUNKS - 3)]
    offsets = [sum(sizes[:c]) for c in range(CHUNKS)]
    pieces = [own_block[offsets[c]:offsets[c] + sizes[c]] for c in range(CHUNKS)]

    odd = list(range(1, count, 2))
    even = list(range(0, count, 2))
    z_down = [(s, s - 2) for s in range(2, count)]
    odd_to_even = [(s, s - 1) for s in odd]
    even_to_odd = [(s, s + 1) for s in even if s + 1 < count]

    even_me = me % 2 == 0
    low = me < 2
    partner = [(j, j ^ 1) for j in range(groups)]
    across = [(j, j ^ 2) for j in range(groups)]

    names = ("two", "one_even", "one_odd", "three_even", "three_odd", "tiles", "first", "results")
    state = {name: [None] * CHUNKS for name in names}

    def finish(c):
        blocks = jnp.concatenate([
            pieces[c],
            state["one_even"][c] + state["one_odd"][c],
            state["two"][c],
            state["three_even"][c] + state["three_odd"][c],
        ], axis=0)
        gram = jnp.einsum("ab,cb->ac", own_block, blocks, preferred_element_type=jnp.float32)
        step = sizes[c]
        tiles = [gram[:, k * step:(k + 1) * step] for k in range(BAND + 1)]
        state["tiles"][c] = tiles
        if c == CHUNKS - 1:
            outgoing = []
            for i in [0] + flips:
                target = tiles[0]
                for k in range(1, groups):
                    target = jnp.where(jnp.bitwise_xor(me, i) == k, tiles[k], target)
                outgoing.append(target)
            arrived = [outgoing[0]] + [
                lax.ppermute(outgoing[i], "samp", [(j, j ^ i) for j in range(groups)]) for i in flips]
            state["results"][c] = added(arrived)
        else:
            payload = jnp.where(even_me, jnp.concatenate([tiles[1], tiles[3]], axis=1),
                                jnp.concatenate([tiles[0], tiles[2]], axis=1))
            state["first"][c] = lax.ppermute(payload, "samp", partner)

    def pick(c, a, b, d, e):
        t = state["tiles"][c]
        return jnp.where(low, jnp.where(even_me, t[a], t[b]), jnp.where(even_me, t[d], t[e]))

    def second_level(c):
        step = sizes[c]
        got = state["first"][c]
        mine = jnp.where(low, got[:, :step], got[:, step:])
        onward = jnp.where(low, got[:, step:], got[:, :step])
        last = lax.ppermute(pick(c, 2, 3, 0, 1) + onward, "samp", across)
        state["results"][c] = pick(c, 0, 1, 2, 3) + mine + last

    for t in range(CHUNKS + 3):
        new = t if t < CHUNKS else None
        second = t - 1 if 0 <= t - 1 < CHUNKS else None
        third = t - 2 if 0 <= t - 2 < CHUNKS else None
        if new is not None or third is not None:
            sent = moved(joined([pieces[new] if new is not None else None,
                                 state["one_odd"][third] if third is not None else None]), z_down)
            if new is not None:
                state["two"][new] = sent[:sizes[new]]
            if third is not None:
                state["three_odd"][third] = sent[-sizes[third]:]
        if new is not None or second is not None:
            sent = moved(joined([pieces[new] if new is not None else None,
                                 state["two"][second] if second is not None else None]), odd_to_even)
            if new is not None:
                state["one_even"][new] = sent[:sizes[new]]
            if second is not None:
                state["three_even"][second] = sent[-sizes[second]:]
        if second is not None:
            state["one_odd"][second] = moved(state["two"][second], even_to_odd)
        if 0 <= t - 3 < CHUNKS:
            finish(t - 3)
        if 0 <= t - 4 < CHUNKS - 1:
            second_level(t - 4)
        flat, tree = jax.tree.flatten(state)
        following = pieces[t + 1] if t + 1 < CHUNKS else own_block[:8]
        flat, following = lax.optimization_barrier((flat, following))
        state = {k: list(v) for k, v in jax.tree.unflatten(tree, flat).items()}
        if t + 1 < CHUNKS:
            pieces[t + 1] = following
    summed = jnp.concatenate(state["results"], axis=1)
    return summed / total


def solution(mesh):
    return jax.shard_map(
        local,
        mesh=mesh,
        in_specs=(P("snp", "samp"),),
        out_specs=P("snp", "samp"),
        check_vma=False,
    )
```

```python
import jax
import jax.numpy as jnp
from jax import lax
from jax.sharding import PartitionSpec as P

BAND = 3
CHUNKS = 8


def moved(value, pairs):
    return lax.ppermute(value, "snp", pairs)


def standardize(values, sums, squares, total):
    mean = sums / total
    variance = squares / total - mean * mean
    return ((values - mean[:, None]) * lax.rsqrt(variance + 1e-05)[:, None]).astype(jnp.bfloat16)


def local_moments(values):
    return (jnp.sum(values, axis=1), jnp.sum(values * values, axis=1))


def joined(parts):
    parts = [p for p in parts if p is not None]
    return parts[0] if len(parts) == 1 else jnp.concatenate(parts, axis=0)


def local(dosages):
    total = dosages.shape[1] * lax.axis_size("samp")
    count = lax.axis_size("snp")
    groups = lax.axis_size("samp")
    me = lax.axis_index("samp")
    flips = list(range(1, groups))

    def choose(values):
        ordered = []
        for k in range(groups):
            pick = values[0]
            for i in flips:
                pick = jnp.where(jnp.bitwise_xor(me, i) == k, values[i], pick)
            ordered.append(pick)
        return ordered

    def added(values):
        ordered = choose(values)
        result = ordered[0]
        for part in ordered[1:]:
            result = result + part
        return result

    def standard_rows(values):
        moments = jnp.stack(local_moments(values))
        summed = added(
            [moments] + [lax.ppermute(moments, "samp", [(j, j ^ i) for j in range(groups)]) for i in flips])
        return standardize(values, summed[0], summed[1], total)

    rows = dosages.shape[0]
    step = rows // CHUNKS
    first_piece = standard_rows(dosages[:step])
    rest = standard_rows(dosages[step:])
    own_block = jnp.concatenate([first_piece, rest], axis=0)
    pieces = [first_piece] + [rest[(c - 1) * step:c * step] for c in range(1, CHUNKS)]

    odd = list(range(1, count, 2))
    even = list(range(0, count, 2))
    z_down = [(s, s - 2) for s in range(2, count)]
    odd_to_even = [(s, s - 1) for s in odd]
    even_to_odd = [(s, s + 1) for s in even if s + 1 < count]

    even_me = me % 2 == 0
    low = me < 2
    partner = [(j, j ^ 1) for j in range(groups)]
    across = [(j, j ^ 2) for j in range(groups)]

    names = ("two", "one_even", "one_odd", "three_even", "three_odd", "tiles", "first", "results")
    state = {name: [None] * CHUNKS for name in names}

    def finish(c):
        blocks = jnp.concatenate([
            pieces[c],
            state["one_even"][c] + state["one_odd"][c],
            state["two"][c],
            state["three_even"][c] + state["three_odd"][c],
        ], axis=0)
        gram = jnp.einsum("ab,cb->ac", own_block, blocks, preferred_element_type=jnp.float32)
        tiles = [gram[:, k * step:(k + 1) * step] for k in range(BAND + 1)]
        state["tiles"][c] = tiles
        if c == CHUNKS - 1:
            outgoing = []
            for i in [0] + flips:
                target = tiles[0]
                for k in range(1, groups):
                    target = jnp.where(jnp.bitwise_xor(me, i) == k, tiles[k], target)
                outgoing.append(target)
            arrived = [outgoing[0]] + [
                lax.ppermute(outgoing[i], "samp", [(j, j ^ i) for j in range(groups)]) for i in flips]
            state["results"][c] = added(arrived)
        else:
            payload = jnp.where(even_me, jnp.concatenate([tiles[1], tiles[3]], axis=1),
                                jnp.concatenate([tiles[0], tiles[2]], axis=1))
            state["first"][c] = lax.ppermute(payload, "samp", partner)

    def pick(c, a, b, d, e):
        t = state["tiles"][c]
        return jnp.where(low, jnp.where(even_me, t[a], t[b]), jnp.where(even_me, t[d], t[e]))

    def second_level(c):
        got = state["first"][c]
        mine = jnp.where(low, got[:, :step], got[:, step:])
        onward = jnp.where(low, got[:, step:], got[:, :step])
        last = lax.ppermute(pick(c, 2, 3, 0, 1) + onward, "samp", across)
        state["results"][c] = pick(c, 0, 1, 2, 3) + mine + last

    for t in range(CHUNKS + 3):
        new = t if t < CHUNKS else None
        second = t - 1 if 0 <= t - 1 < CHUNKS else None
        third = t - 2 if 0 <= t - 2 < CHUNKS else None
        if new is not None or third is not None:
            sent = moved(joined([pieces[new] if new is not None else None,
                                 state["one_odd"][third] if third is not None else None]), z_down)
            if new is not None:
                state["two"][new] = sent[:step]
            if third is not None:
                state["three_odd"][third] = sent[-step:]
        if new is not None or second is not None:
            sent = moved(joined([pieces[new] if new is not None else None,
                                 state["two"][second] if second is not None else None]), odd_to_even)
            if new is not None:
                state["one_even"][new] = sent[:step]
            if second is not None:
                state["three_even"][second] = sent[-step:]
        if second is not None:
            state["one_odd"][second] = moved(state["two"][second], even_to_odd)
        if 0 <= t - 3 < CHUNKS:
            finish(t - 3)
        if 0 <= t - 4 < CHUNKS - 1:
            second_level(t - 4)
        flat, tree = jax.tree.flatten(state)
        following = pieces[t + 1] if t + 1 < CHUNKS else own_block[:8]
        flat, following = lax.optimization_barrier((flat, following))
        state = {k: list(v) for k, v in jax.tree.unflatten(tree, flat).items()}
        if t + 1 < CHUNKS:
            pieces[t + 1] = following
    summed = jnp.concatenate(state["results"], axis=1)
    return summed / total


def solution(mesh):
    return jax.shard_map(
        local,
        mesh=mesh,
        in_specs=(P("snp", "samp"),),
        out_specs=P("snp", "samp"),
        check_vma=False,
    )
```

```python
import jax
import jax.numpy as jnp
from jax import lax
from jax.sharding import PartitionSpec as P

BAND = 3
CHUNKS = 8


def moved(value, pairs):
    return lax.ppermute(value, "snp", pairs)


def standardize(values, sums, squares, total):
    mean = sums / total
    variance = squares / total - mean * mean
    return ((values - mean[:, None]) * lax.rsqrt(variance + 1e-05)[:, None]).astype(jnp.bfloat16)


def local_moments(values):
    return (jnp.sum(values, axis=1), jnp.sum(values * values, axis=1))


def joined(parts):
    parts = [p for p in parts if p is not None]
    return parts[0] if len(parts) == 1 else jnp.concatenate(parts, axis=0)


def local(dosages):
    total = dosages.shape[1] * lax.axis_size("samp")
    count = lax.axis_size("snp")
    groups = lax.axis_size("samp")
    me = lax.axis_index("samp")
    flips = list(range(1, groups))

    def choose(values):
        ordered = []
        for k in range(groups):
            pick = values[0]
            for i in flips:
                pick = jnp.where(jnp.bitwise_xor(me, i) == k, values[i], pick)
            ordered.append(pick)
        return ordered

    def added(values):
        ordered = choose(values)
        result = ordered[0]
        for part in ordered[1:]:
            result = result + part
        return result

    def standard_rows(values):
        moments = jnp.stack(local_moments(values))
        summed = added(
            [moments] + [lax.ppermute(moments, "samp", [(j, j ^ i) for j in range(groups)]) for i in flips])
        return standardize(values, summed[0], summed[1], total)

    rows = dosages.shape[0]
    step = rows // CHUNKS
    first_piece = standard_rows(dosages[:step])
    first_piece, later = lax.optimization_barrier((first_piece, dosages[step:]))
    rest = standard_rows(later)
    own_block = jnp.concatenate([first_piece, rest], axis=0)
    pieces = [first_piece] + [rest[(c - 1) * step:c * step] for c in range(1, CHUNKS)]

    odd = list(range(1, count, 2))
    even = list(range(0, count, 2))
    z_down = [(s, s - 2) for s in range(2, count)]
    odd_to_even = [(s, s - 1) for s in odd]
    even_to_odd = [(s, s + 1) for s in even if s + 1 < count]

    even_me = me % 2 == 0
    low = me < 2
    partner = [(j, j ^ 1) for j in range(groups)]
    across = [(j, j ^ 2) for j in range(groups)]

    names = ("two", "one_even", "one_odd", "three_even", "three_odd", "tiles", "first", "results")
    state = {name: [None] * CHUNKS for name in names}

    def finish(c):
        blocks = jnp.concatenate([
            pieces[c],
            state["one_even"][c] + state["one_odd"][c],
            state["two"][c],
            state["three_even"][c] + state["three_odd"][c],
        ], axis=0)
        gram = jnp.einsum("ab,cb->ac", own_block, blocks, preferred_element_type=jnp.float32)
        tiles = [gram[:, k * step:(k + 1) * step] for k in range(BAND + 1)]
        state["tiles"][c] = tiles
        if c == CHUNKS - 1:
            outgoing = []
            for i in [0] + flips:
                target = tiles[0]
                for k in range(1, groups):
                    target = jnp.where(jnp.bitwise_xor(me, i) == k, tiles[k], target)
                outgoing.append(target)
            arrived = [outgoing[0]] + [
                lax.ppermute(outgoing[i], "samp", [(j, j ^ i) for j in range(groups)]) for i in flips]
            state["results"][c] = added(arrived)
        else:
            payload = jnp.where(even_me, jnp.concatenate([tiles[1], tiles[3]], axis=1),
                                jnp.concatenate([tiles[0], tiles[2]], axis=1))
            state["first"][c] = lax.ppermute(payload, "samp", partner)

    def pick(c, a, b, d, e):
        t = state["tiles"][c]
        return jnp.where(low, jnp.where(even_me, t[a], t[b]), jnp.where(even_me, t[d], t[e]))

    def second_level(c):
        got = state["first"][c]
        mine = jnp.where(low, got[:, :step], got[:, step:])
        onward = jnp.where(low, got[:, step:], got[:, :step])
        last = lax.ppermute(pick(c, 2, 3, 0, 1) + onward, "samp", across)
        state["results"][c] = pick(c, 0, 1, 2, 3) + mine + last

    for t in range(CHUNKS + 3):
        new = t if t < CHUNKS else None
        second = t - 1 if 0 <= t - 1 < CHUNKS else None
        third = t - 2 if 0 <= t - 2 < CHUNKS else None
        if new is not None or third is not None:
            sent = moved(joined([pieces[new] if new is not None else None,
                                 state["one_odd"][third] if third is not None else None]), z_down)
            if new is not None:
                state["two"][new] = sent[:step]
            if third is not None:
                state["three_odd"][third] = sent[-step:]
        if new is not None or second is not None:
            sent = moved(joined([pieces[new] if new is not None else None,
                                 state["two"][second] if second is not None else None]), odd_to_even)
            if new is not None:
                state["one_even"][new] = sent[:step]
            if second is not None:
                state["three_even"][second] = sent[-step:]
        if second is not None:
            state["one_odd"][second] = moved(state["two"][second], even_to_odd)
        if 0 <= t - 3 < CHUNKS:
            finish(t - 3)
        if 0 <= t - 4 < CHUNKS - 1:
            second_level(t - 4)
        flat, tree = jax.tree.flatten(state)
        following = pieces[t + 1] if t + 1 < CHUNKS else own_block[:8]
        flat, following = lax.optimization_barrier((flat, following))
        state = {k: list(v) for k, v in jax.tree.unflatten(tree, flat).items()}
        if t + 1 < CHUNKS:
            pieces[t + 1] = following
    summed = jnp.concatenate(state["results"], axis=1)
    return summed / total


def solution(mesh):
    return jax.shard_map(
        local,
        mesh=mesh,
        in_specs=(P("snp", "samp"),),
        out_specs=P("snp", "samp"),
        check_vma=False,
    )
```

```python
import jax
import jax.numpy as jnp
from jax import lax
from jax.sharding import PartitionSpec as P

BAND = 3
CHUNKS = 8


def moved(value, pairs):
    return lax.ppermute(value, "snp", pairs)


def standardize(values, sums, squares, total):
    mean = sums / total
    variance = squares / total - mean * mean
    return ((values - mean[:, None]) * lax.rsqrt(variance + 1e-05)[:, None]).astype(jnp.bfloat16)


def local_moments(values):
    return (jnp.sum(values, axis=1), jnp.sum(values * values, axis=1))


def joined(parts):
    parts = [p for p in parts if p is not None]
    return parts[0] if len(parts) == 1 else jnp.concatenate(parts, axis=0)


def local(dosages):
    total = dosages.shape[1] * lax.axis_size("samp")
    count = lax.axis_size("snp")
    groups = lax.axis_size("samp")
    me = lax.axis_index("samp")
    flips = list(range(1, groups))

    def choose(values):
        ordered = []
        for k in range(groups):
            pick = values[0]
            for i in flips:
                pick = jnp.where(jnp.bitwise_xor(me, i) == k, values[i], pick)
            ordered.append(pick)
        return ordered

    def added(values):
        ordered = choose(values)
        result = ordered[0]
        for part in ordered[1:]:
            result = result + part
        return result

    def standard_rows(values):
        moments = jnp.stack(local_moments(values))
        summed = added(
            [moments] + [lax.ppermute(moments, "samp", [(j, j ^ i) for j in range(groups)]) for i in flips])
        return standardize(values, summed[0], summed[1], total)

    rows = dosages.shape[0]
    step = rows // CHUNKS
    first_piece = standard_rows(dosages[:step])
    first_piece, later = lax.optimization_barrier((first_piece, dosages))
    rest = standard_rows(later[step:])
    own_block = jnp.concatenate([first_piece, rest], axis=0)
    pieces = [first_piece] + [rest[(c - 1) * step:c * step] for c in range(1, CHUNKS)]

    odd = list(range(1, count, 2))
    even = list(range(0, count, 2))
    z_down = [(s, s - 2) for s in range(2, count)]
    odd_to_even = [(s, s - 1) for s in odd]
    even_to_odd = [(s, s + 1) for s in even if s + 1 < count]

    even_me = me % 2 == 0
    low = me < 2
    partner = [(j, j ^ 1) for j in range(groups)]
    across = [(j, j ^ 2) for j in range(groups)]

    names = ("two", "one_even", "one_odd", "three_even", "three_odd", "tiles", "first", "results")
    state = {name: [None] * CHUNKS for name in names}

    def finish(c):
        blocks = jnp.concatenate([
            pieces[c],
            state["one_even"][c] + state["one_odd"][c],
            state["two"][c],
            state["three_even"][c] + state["three_odd"][c],
        ], axis=0)
        gram = jnp.einsum("ab,cb->ac", own_block, blocks, preferred_element_type=jnp.float32)
        tiles = [gram[:, k * step:(k + 1) * step] for k in range(BAND + 1)]
        state["tiles"][c] = tiles
        if c == CHUNKS - 1:
            outgoing = []
            for i in [0] + flips:
                target = tiles[0]
                for k in range(1, groups):
                    target = jnp.where(jnp.bitwise_xor(me, i) == k, tiles[k], target)
                outgoing.append(target)
            arrived = [outgoing[0]] + [
                lax.ppermute(outgoing[i], "samp", [(j, j ^ i) for j in range(groups)]) for i in flips]
            state["results"][c] = added(arrived)
        else:
            payload = jnp.where(even_me, jnp.concatenate([tiles[1], tiles[3]], axis=1),
                                jnp.concatenate([tiles[0], tiles[2]], axis=1))
            state["first"][c] = lax.ppermute(payload, "samp", partner)

    def pick(c, a, b, d, e):
        t = state["tiles"][c]
        return jnp.where(low, jnp.where(even_me, t[a], t[b]), jnp.where(even_me, t[d], t[e]))

    def second_level(c):
        got = state["first"][c]
        mine = jnp.where(low, got[:, :step], got[:, step:])
        onward = jnp.where(low, got[:, step:], got[:, :step])
        last = lax.ppermute(pick(c, 2, 3, 0, 1) + onward, "samp", across)
        state["results"][c] = pick(c, 0, 1, 2, 3) + mine + last

    for t in range(CHUNKS + 3):
        new = t if t < CHUNKS else None
        second = t - 1 if 0 <= t - 1 < CHUNKS else None
        third = t - 2 if 0 <= t - 2 < CHUNKS else None
        if new is not None or third is not None:
            sent = moved(joined([pieces[new] if new is not None else None,
                                 state["one_odd"][third] if third is not None else None]), z_down)
            if new is not None:
                state["two"][new] = sent[:step]
            if third is not None:
                state["three_odd"][third] = sent[-step:]
        if new is not None or second is not None:
            sent = moved(joined([pieces[new] if new is not None else None,
                                 state["two"][second] if second is not None else None]), odd_to_even)
            if new is not None:
                state["one_even"][new] = sent[:step]
            if second is not None:
                state["three_even"][second] = sent[-step:]
        if second is not None:
            state["one_odd"][second] = moved(state["two"][second], even_to_odd)
        if 0 <= t - 3 < CHUNKS:
            finish(t - 3)
        if 0 <= t - 4 < CHUNKS - 1:
            second_level(t - 4)
        flat, tree = jax.tree.flatten(state)
        following = pieces[t + 1] if t + 1 < CHUNKS else own_block[:8]
        flat, following = lax.optimization_barrier((flat, following))
        state = {k: list(v) for k, v in jax.tree.unflatten(tree, flat).items()}
        if t + 1 < CHUNKS:
            pieces[t + 1] = following
    summed = jnp.concatenate(state["results"], axis=1)
    return summed / total


def solution(mesh):
    return jax.shard_map(
        local,
        mesh=mesh,
        in_specs=(P("snp", "samp"),),
        out_specs=P("snp", "samp"),
        check_vma=False,
    )
```

```python
import jax
import jax.numpy as jnp
from jax import lax
from jax.sharding import PartitionSpec as P

BAND = 3
CHUNKS = 8


def moved(value, pairs):
    return lax.ppermute(value, "snp", pairs)


def standardize(values, sums, squares, total):
    mean = sums / total
    variance = squares / total - mean * mean
    return ((values - mean[:, None]) * lax.rsqrt(variance + 1e-05)[:, None]).astype(jnp.bfloat16)


def local_moments(values):
    return (jnp.sum(values, axis=1), jnp.sum(values * values, axis=1))


def joined(parts):
    parts = [p for p in parts if p is not None]
    return parts[0] if len(parts) == 1 else jnp.concatenate(parts, axis=0)


def local(dosages):
    total = dosages.shape[1] * lax.axis_size("samp")
    count = lax.axis_size("snp")
    groups = lax.axis_size("samp")
    me = lax.axis_index("samp")
    flips = list(range(1, groups))

    def choose(values):
        ordered = []
        for k in range(groups):
            pick = values[0]
            for i in flips:
                pick = jnp.where(jnp.bitwise_xor(me, i) == k, values[i], pick)
            ordered.append(pick)
        return ordered

    def added(values):
        ordered = choose(values)
        result = ordered[0]
        for part in ordered[1:]:
            result = result + part
        return result

    def standard_rows(values):
        moments = jnp.stack(local_moments(values))
        summed = added(
            [moments] + [lax.ppermute(moments, "samp", [(j, j ^ i) for j in range(groups)]) for i in flips])
        return standardize(values, summed[0], summed[1], total)

    rows = dosages.shape[0]
    step = rows // CHUNKS
    first_piece = standard_rows(dosages[:step])
    rest = standard_rows(dosages[step:])
    own_block = jnp.concatenate([first_piece, rest], axis=0)
    pieces = [first_piece] + [rest[(c - 1) * step:c * step] for c in range(1, CHUNKS)]

    odd = list(range(1, count, 2))
    even = list(range(0, count, 2))
    z_down = [(s, s - 2) for s in range(2, count)]
    swap = [(s, s - 1) for s in odd] + [(s, s + 1) for s in even if s + 1 < count]
    even_snp = lax.axis_index("snp") % 2 == 0

    even_me = me % 2 == 0
    low = me < 2
    partner = [(j, j ^ 1) for j in range(groups)]
    across = [(j, j ^ 2) for j in range(groups)]

    names = ("two", "one", "three_even", "three_odd", "tiles", "first", "results")
    state = {name: [None] * CHUNKS for name in names}

    def finish(c):
        blocks = jnp.concatenate([
            pieces[c],
            state["one"][c],
            state["two"][c],
            jnp.where(even_snp, state["three_even"][c], state["three_odd"][c]),
        ], axis=0)
        gram = jnp.einsum("ab,cb->ac", own_block, blocks, preferred_element_type=jnp.float32)
        tiles = [gram[:, k * step:(k + 1) * step] for k in range(BAND + 1)]
        state["tiles"][c] = tiles
        if c == CHUNKS - 1:
            outgoing = []
            for i in [0] + flips:
                target = tiles[0]
                for k in range(1, groups):
                    target = jnp.where(jnp.bitwise_xor(me, i) == k, tiles[k], target)
                outgoing.append(target)
            arrived = [outgoing[0]] + [
                lax.ppermute(outgoing[i], "samp", [(j, j ^ i) for j in range(groups)]) for i in flips]
            state["results"][c] = added(arrived)
        else:
            payload = jnp.where(even_me, jnp.concatenate([tiles[1], tiles[3]], axis=1),
                                jnp.concatenate([tiles[0], tiles[2]], axis=1))
            state["first"][c] = lax.ppermute(payload, "samp", partner)

    def pick(c, a, b, d, e):
        t = state["tiles"][c]
        return jnp.where(low, jnp.where(even_me, t[a], t[b]), jnp.where(even_me, t[d], t[e]))

    def second_level(c):
        got = state["first"][c]
        mine = jnp.where(low, got[:, :step], got[:, step:])
        onward = jnp.where(low, got[:, step:], got[:, :step])
        last = lax.ppermute(pick(c, 2, 3, 0, 1) + onward, "samp", across)
        state["results"][c] = pick(c, 0, 1, 2, 3) + mine + last

    for t in range(CHUNKS + 3):
        new = t if t < CHUNKS else None
        second = t - 1 if 0 <= t - 1 < CHUNKS else None
        third = t - 2 if 0 <= t - 2 < CHUNKS else None
        if new is not None or third is not None:
            sent = moved(joined([pieces[new] if new is not None else None,
                                 state["one"][third] if third is not None else None]), z_down)
            if new is not None:
                state["two"][new] = sent[:step]
            if third is not None:
                state["three_odd"][third] = sent[-step:]
        if new is not None or second is not None:
            sent = moved(joined([pieces[new] if new is not None else None,
                                 state["two"][second] if second is not None else None]), swap)
            if new is not None:
                state["one"][new] = sent[:step]
            if second is not None:
                state["three_even"][second] = sent[-step:]
                state["one"][second] = jnp.where(even_snp, state["one"][second], sent[-step:])
        if 0 <= t - 3 < CHUNKS:
            finish(t - 3)
        if 0 <= t - 4 < CHUNKS - 1:
            second_level(t - 4)
        flat, tree = jax.tree.flatten(state)
        following = pieces[t + 1] if t + 1 < CHUNKS else own_block[:8]
        flat, following = lax.optimization_barrier((flat, following))
        state = {k: list(v) for k, v in jax.tree.unflatten(tree, flat).items()}
        if t + 1 < CHUNKS:
            pieces[t + 1] = following
    summed = jnp.concatenate(state["results"], axis=1)
    return summed / total


def solution(mesh):
    return jax.shard_map(
        local,
        mesh=mesh,
        in_specs=(P("snp", "samp"),),
        out_specs=P("snp", "samp"),
        check_vma=False,
    )
```

```python
import jax
import jax.numpy as jnp
from jax import lax
from jax.sharding import PartitionSpec as P

BAND = 3
CHUNKS = 8


def moved(value, pairs):
    return lax.ppermute(value, "snp", pairs)


def standardize(values, sums, squares, total):
    mean = sums / total
    variance = squares / total - mean * mean
    return ((values - mean[:, None]) * lax.rsqrt(variance + 1e-05)[:, None]).astype(jnp.bfloat16)


def local_moments(values):
    return (jnp.sum(values, axis=1), jnp.sum(values * values, axis=1))


def joined(parts):
    parts = [p for p in parts if p is not None]
    return parts[0] if len(parts) == 1 else jnp.concatenate(parts, axis=0)


def local(dosages):
    total = dosages.shape[1] * lax.axis_size("samp")
    count = lax.axis_size("snp")
    groups = lax.axis_size("samp")
    me = lax.axis_index("samp")
    flips = list(range(1, groups))

    def choose(values):
        ordered = []
        for k in range(groups):
            pick = values[0]
            for i in flips:
                pick = jnp.where(jnp.bitwise_xor(me, i) == k, values[i], pick)
            ordered.append(pick)
        return ordered

    def added(values):
        ordered = choose(values)
        result = ordered[0]
        for part in ordered[1:]:
            result = result + part
        return result

    def standard_rows(values):
        moments = jnp.stack(local_moments(values))
        summed = added(
            [moments] + [lax.ppermute(moments, "samp", [(j, j ^ i) for j in range(groups)]) for i in flips])
        return standardize(values, summed[0], summed[1], total)

    rows = dosages.shape[0]
    step = rows // CHUNKS
    first_piece = standard_rows(dosages[:step])
    rest = standard_rows(dosages[step:])
    own_block = jnp.concatenate([first_piece, rest], axis=0)
    pieces = [first_piece] + [rest[(c - 1) * step:c * step] for c in range(1, CHUNKS)]

    odd = list(range(1, count, 2))
    even = list(range(0, count, 2))
    z_down = [(s, s - 2) for s in range(2, count)]
    swap = [(s, s - 1) for s in odd] + [(s, s + 1) for s in even if s + 1 < count]
    even_snp = lax.axis_index("snp") % 2 == 0

    even_me = me % 2 == 0
    low = me < 2
    partner = [(j, j ^ 1) for j in range(groups)]
    across = [(j, j ^ 2) for j in range(groups)]

    names = ("two", "swapped", "one", "three", "tiles", "first", "results")
    state = {name: [None] * (CHUNKS + 1) for name in names}

    def finish(c):
        blocks = jnp.concatenate([
            pieces[c],
            state["one"][c],
            state["two"][c],
            state["three"][c],
        ], axis=0)
        gram = jnp.einsum("ab,cb->ac", own_block, blocks, preferred_element_type=jnp.float32)
        tiles = [gram[:, k * step:(k + 1) * step] for k in range(BAND + 1)]
        state["tiles"][c] = tiles
        if c == CHUNKS - 1:
            outgoing = []
            for i in [0] + flips:
                target = tiles[0]
                for k in range(1, groups):
                    target = jnp.where(jnp.bitwise_xor(me, i) == k, tiles[k], target)
                outgoing.append(target)
            arrived = [outgoing[0]] + [
                lax.ppermute(outgoing[i], "samp", [(j, j ^ i) for j in range(groups)]) for i in flips]
            state["results"][c] = added(arrived)
        else:
            payload = jnp.where(even_me, jnp.concatenate([tiles[1], tiles[3]], axis=1),
                                jnp.concatenate([tiles[0], tiles[2]], axis=1))
            state["first"][c] = lax.ppermute(payload, "samp", partner)

    def pick(c, a, b, d, e):
        t = state["tiles"][c]
        return jnp.where(low, jnp.where(even_me, t[a], t[b]), jnp.where(even_me, t[d], t[e]))

    def second_level(c):
        got = state["first"][c]
        mine = jnp.where(low, got[:, :step], got[:, step:])
        onward = jnp.where(low, got[:, step:], got[:, :step])
        last = lax.ppermute(pick(c, 2, 3, 0, 1) + onward, "samp", across)
        state["results"][c] = pick(c, 0, 1, 2, 3) + mine + last

    for t in range(CHUNKS + 3):
        new = t if t < CHUNKS else None
        second = t - 1 if 0 <= t - 1 < CHUNKS else None
        third = t - 2 if 0 <= t - 2 < CHUNKS else None
        if new is not None or third is not None:
            sent = moved(joined([pieces[new] if new is not None else None,
                                 state["one"][third] if third is not None else None]), z_down)
            if new is not None:
                state["two"][new] = sent[:step]
            if third is not None:
                state["three"][third] = sent[-step:]
        if new is not None or second is not None:
            if new is not None and second is not None:
                payload = jnp.where(even_snp, state["two"][second], pieces[new])
            else:
                payload = pieces[new] if new is not None else state["two"][second]
            state["swapped"][t] = moved(payload, swap)
        if second is not None:
            state["one"][second] = jnp.where(even_snp, state["swapped"][second], state["swapped"][t])
        if 0 <= t - 3 < CHUNKS:
            finish(t - 3)
        if 0 <= t - 4 < CHUNKS - 1:
            second_level(t - 4)
        flat, tree = jax.tree.flatten(state)
        following = pieces[t + 1] if t + 1 < CHUNKS else own_block[:8]
        flat, following = lax.optimization_barrier((flat, following))
        state = {k: list(v) for k, v in jax.tree.unflatten(tree, flat).items()}
        if t + 1 < CHUNKS:
            pieces[t + 1] = following
    summed = jnp.concatenate(state["results"][:CHUNKS], axis=1)
    return summed / total


def solution(mesh):
    return jax.shard_map(
        local,
        mesh=mesh,
        in_specs=(P("snp", "samp"),),
        out_specs=P("snp", "samp"),
        check_vma=False,
    )
```

```python
import jax
import jax.numpy as jnp
from jax import lax
from jax.sharding import PartitionSpec as P

BAND = 3
CHUNKS = 8


def moved(value, pairs):
    return lax.ppermute(value, "snp", pairs)


def standardize(values, sums, squares, total):
    mean = sums / total
    variance = squares / total - mean * mean
    return ((values - mean[:, None]) * lax.rsqrt(variance + 1e-05)[:, None]).astype(jnp.bfloat16)


def local_moments(values):
    return (jnp.sum(values, axis=1), jnp.sum(values * values, axis=1))


def joined(parts):
    parts = [p for p in parts if p is not None]
    return parts[0] if len(parts) == 1 else jnp.concatenate(parts, axis=0)


def local(dosages):
    total = dosages.shape[1] * lax.axis_size("samp")
    count = lax.axis_size("snp")
    groups = lax.axis_size("samp")
    me = lax.axis_index("samp")
    flips = list(range(1, groups))

    def choose(values):
        ordered = []
        for k in range(groups):
            pick = values[0]
            for i in flips:
                pick = jnp.where(jnp.bitwise_xor(me, i) == k, values[i], pick)
            ordered.append(pick)
        return ordered

    def added(values):
        ordered = choose(values)
        result = ordered[0]
        for part in ordered[1:]:
            result = result + part
        return result

    def standard_rows(values):
        moments = jnp.stack(local_moments(values))
        summed = added(
            [moments] + [lax.ppermute(moments, "samp", [(j, j ^ i) for j in range(groups)]) for i in flips])
        return standardize(values, summed[0], summed[1], total)

    rows = dosages.shape[0]
    step = rows // CHUNKS
    first_piece = standard_rows(dosages[:step])
    rest = standard_rows(dosages[step:])
    own_block = jnp.concatenate([first_piece, rest], axis=0)
    pieces = [first_piece] + [rest[(c - 1) * step:c * step] for c in range(1, CHUNKS)]

    odd = list(range(1, count, 2))
    even = list(range(0, count, 2))
    z_down = [(s, s - 2) for s in range(2, count)]
    swap = [(s, s - 1) for s in odd] + [(s, s + 1) for s in even if s + 1 < count]
    even_snp = lax.axis_index("snp") % 2 == 0

    even_me = me % 2 == 0
    low = me < 2
    partner = [(j, j ^ 1) for j in range(groups)]
    across = [(j, j ^ 2) for j in range(groups)]

    names = ("two", "swapped", "one", "three", "tiles", "first", "results")
    state = {name: [None] * (CHUNKS + 1) for name in names}

    def finish(c):
        blocks = jnp.concatenate([
            pieces[c],
            state["one"][c],
            state["two"][c],
            state["three"][c],
        ], axis=0)
        gram = jnp.einsum("ab,cb->ac", own_block, blocks, preferred_element_type=jnp.float32)
        tiles = [gram[:, k * step:(k + 1) * step] for k in range(BAND + 1)]
        state["tiles"][c] = tiles
        payload = jnp.where(even_me, jnp.concatenate([tiles[1], tiles[3]], axis=1),
                            jnp.concatenate([tiles[0], tiles[2]], axis=1))
        state["first"][c] = lax.ppermute(payload, "samp", partner)
        if c == CHUNKS - 1:
            second_level(c)

    def pick(c, a, b, d, e):
        t = state["tiles"][c]
        return jnp.where(low, jnp.where(even_me, t[a], t[b]), jnp.where(even_me, t[d], t[e]))

    def second_level(c):
        got = state["first"][c]
        mine = jnp.where(low, got[:, :step], got[:, step:])
        onward = jnp.where(low, got[:, step:], got[:, :step])
        last = lax.ppermute(pick(c, 2, 3, 0, 1) + onward, "samp", across)
        state["results"][c] = pick(c, 0, 1, 2, 3) + mine + last

    for t in range(CHUNKS + 3):
        new = t if t < CHUNKS else None
        second = t - 1 if 0 <= t - 1 < CHUNKS else None
        third = t - 2 if 0 <= t - 2 < CHUNKS else None
        if new is not None or third is not None:
            sent = moved(joined([pieces[new] if new is not None else None,
                                 state["one"][third] if third is not None else None]), z_down)
            if new is not None:
                state["two"][new] = sent[:step]
            if third is not None:
                state["three"][third] = sent[-step:]
        if new is not None or second is not None:
            if new is not None and second is not None:
                payload = jnp.where(even_snp, state["two"][second], pieces[new])
            else:
                payload = pieces[new] if new is not None else state["two"][second]
            state["swapped"][t] = moved(payload, swap)
        if second is not None:
            state["one"][second] = jnp.where(even_snp, state["swapped"][second], state["swapped"][t])
        if 0 <= t - 3 < CHUNKS:
            finish(t - 3)
        if 0 <= t - 4 < CHUNKS - 1:
            second_level(t - 4)
        flat, tree = jax.tree.flatten(state)
        following = pieces[t + 1] if t + 1 < CHUNKS else own_block[:8]
        flat, following = lax.optimization_barrier((flat, following))
        state = {k: list(v) for k, v in jax.tree.unflatten(tree, flat).items()}
        if t + 1 < CHUNKS:
            pieces[t + 1] = following
    summed = jnp.concatenate(state["results"][:CHUNKS], axis=1)
    return summed / total


def solution(mesh):
    return jax.shard_map(
        local,
        mesh=mesh,
        in_specs=(P("snp", "samp"),),
        out_specs=P("snp", "samp"),
        check_vma=False,
    )
```

```python
import jax
import jax.numpy as jnp
from jax import lax
from jax.sharding import PartitionSpec as P

BAND = 3
CHUNKS = 8


def moved(value, pairs):
    return lax.ppermute(value, "snp", pairs)


def standardize(values, sums, squares, total):
    mean = sums / total
    variance = squares / total - mean * mean
    return ((values - mean[:, None]) * lax.rsqrt(variance + 1e-05)[:, None]).astype(jnp.bfloat16)


def local_moments(values):
    return (jnp.sum(values, axis=1), jnp.sum(values * values, axis=1))


def joined(parts):
    parts = [p for p in parts if p is not None]
    return parts[0] if len(parts) == 1 else jnp.concatenate(parts, axis=0)


def local(dosages):
    total = dosages.shape[1] * lax.axis_size("samp")
    count = lax.axis_size("snp")
    groups = lax.axis_size("samp")
    me = lax.axis_index("samp")
    flips = list(range(1, groups))

    def choose(values):
        ordered = []
        for k in range(groups):
            pick = values[0]
            for i in flips:
                pick = jnp.where(jnp.bitwise_xor(me, i) == k, values[i], pick)
            ordered.append(pick)
        return ordered

    def added(values):
        ordered = choose(values)
        result = ordered[0]
        for part in ordered[1:]:
            result = result + part
        return result

    def standard_rows(values):
        moments = jnp.stack(local_moments(values))
        summed = added(
            [moments] + [lax.ppermute(moments, "samp", [(j, j ^ i) for j in range(groups)]) for i in flips])
        return standardize(values, summed[0], summed[1], total)

    rows = dosages.shape[0]
    step = rows // CHUNKS
    sizes = [step + 16] + [step] * (CHUNKS - 2) + [step - 16]
    offsets = [sum(sizes[:c]) for c in range(CHUNKS)]
    first_piece = standard_rows(dosages[:sizes[0]])
    rest = standard_rows(dosages[sizes[0]:])
    own_block = jnp.concatenate([first_piece, rest], axis=0)
    pieces = [first_piece] + [
        rest[offsets[c] - sizes[0]:offsets[c] - sizes[0] + sizes[c]] for c in range(1, CHUNKS)]

    odd = list(range(1, count, 2))
    even = list(range(0, count, 2))
    z_down = [(s, s - 2) for s in range(2, count)]
    swap = [(s, s - 1) for s in odd] + [(s, s + 1) for s in even if s + 1 < count]
    even_snp = lax.axis_index("snp") % 2 == 0

    even_me = me % 2 == 0
    low = me < 2
    partner = [(j, j ^ 1) for j in range(groups)]
    across = [(j, j ^ 2) for j in range(groups)]

    names = ("two", "swapped", "one", "three", "tiles", "first", "results")
    state = {name: [None] * (CHUNKS + 1) for name in names}

    def finish(c):
        blocks = jnp.concatenate([
            pieces[c],
            state["one"][c],
            state["two"][c],
            state["three"][c],
        ], axis=0)
        gram = jnp.einsum("ab,cb->ac", own_block, blocks, preferred_element_type=jnp.float32)
        size = sizes[c]
        tiles = [gram[:, k * size:(k + 1) * size] for k in range(BAND + 1)]
        state["tiles"][c] = tiles
        payload = jnp.where(even_me, jnp.concatenate([tiles[1], tiles[3]], axis=1),
                            jnp.concatenate([tiles[0], tiles[2]], axis=1))
        state["first"][c] = lax.ppermute(payload, "samp", partner)
        if c == CHUNKS - 1:
            second_level(c)

    def pick(c, a, b, d, e):
        t = state["tiles"][c]
        return jnp.where(low, jnp.where(even_me, t[a], t[b]), jnp.where(even_me, t[d], t[e]))

    def second_level(c):
        got = state["first"][c]
        size = sizes[c]
        mine = jnp.where(low, got[:, :size], got[:, size:])
        onward = jnp.where(low, got[:, size:], got[:, :size])
        last = lax.ppermute(pick(c, 2, 3, 0, 1) + onward, "samp", across)
        state["results"][c] = pick(c, 0, 1, 2, 3) + mine + last

    for t in range(CHUNKS + 3):
        new = t if t < CHUNKS else None
        second = t - 1 if 0 <= t - 1 < CHUNKS else None
        third = t - 2 if 0 <= t - 2 < CHUNKS else None
        if new is not None or third is not None:
            sent = moved(joined([pieces[new] if new is not None else None,
                                 state["one"][third] if third is not None else None]), z_down)
            if new is not None:
                state["two"][new] = sent[:sizes[new]]
            if third is not None:
                state["three"][third] = sent[-sizes[third]:]
        if new is not None or second is not None:
            if new is not None and second is not None:
                height = max(sizes[new], sizes[second])
                padded = [jnp.pad(x, ((0, height - x.shape[0]), (0, 0))) for x in (state["two"][second], pieces[new])]
                payload = jnp.where(even_snp, padded[0], padded[1])
            else:
                payload = pieces[new] if new is not None else state["two"][second]
            state["swapped"][t] = moved(payload, swap)
        if second is not None:
            size = sizes[second]
            state["one"][second] = jnp.where(even_snp, state["swapped"][second][:size], state["swapped"][t][:size])
        if 0 <= t - 3 < CHUNKS:
            finish(t - 3)
        if 0 <= t - 4 < CHUNKS - 1:
            second_level(t - 4)
        flat, tree = jax.tree.flatten(state)
        following = pieces[t + 1] if t + 1 < CHUNKS else own_block[:8]
        flat, following = lax.optimization_barrier((flat, following))
        state = {k: list(v) for k, v in jax.tree.unflatten(tree, flat).items()}
        if t + 1 < CHUNKS:
            pieces[t + 1] = following
    summed = jnp.concatenate(state["results"][:CHUNKS], axis=1)
    return summed / total


def solution(mesh):
    return jax.shard_map(
        local,
        mesh=mesh,
        in_specs=(P("snp", "samp"),),
        out_specs=P("snp", "samp"),
        check_vma=False,
    )
```

```python
import jax
import jax.numpy as jnp
from jax import lax
from jax.sharding import PartitionSpec as P

BAND = 3
CHUNKS = 8


def moved(value, pairs):
    return lax.ppermute(value, "snp", pairs)


def standardize(values, sums, squares, total):
    mean = sums / total
    variance = squares / total - mean * mean
    return ((values - mean[:, None]) * lax.rsqrt(variance + 1e-05)[:, None]).astype(jnp.bfloat16)


def local_moments(values):
    return (jnp.sum(values, axis=1), jnp.sum(values * values, axis=1))


def joined(parts):
    parts = [p for p in parts if p is not None]
    return parts[0] if len(parts) == 1 else jnp.concatenate(parts, axis=0)


def local(dosages):
    total = dosages.shape[1] * lax.axis_size("samp")
    count = lax.axis_size("snp")
    groups = lax.axis_size("samp")
    me = lax.axis_index("samp")
    flips = list(range(1, groups))

    def choose(values):
        ordered = []
        for k in range(groups):
            pick = values[0]
            for i in flips:
                pick = jnp.where(jnp.bitwise_xor(me, i) == k, values[i], pick)
            ordered.append(pick)
        return ordered

    def added(values):
        ordered = choose(values)
        result = ordered[0]
        for part in ordered[1:]:
            result = result + part
        return result

    def standard_rows(values):
        moments = jnp.stack(local_moments(values))
        summed = added(
            [moments] + [lax.ppermute(moments, "samp", [(j, j ^ i) for j in range(groups)]) for i in flips])
        return standardize(values, summed[0], summed[1], total)

    rows = dosages.shape[0]
    step = rows // CHUNKS
    sizes = [step + 16] + [step] * (CHUNKS - 2) + [step - 16]
    offsets = [sum(sizes[:c]) for c in range(CHUNKS)]
    first_piece = standard_rows(dosages[:sizes[0]])
    rest = standard_rows(dosages[sizes[0]:])
    own_block = jnp.concatenate([first_piece, rest], axis=0)
    pieces = [first_piece] + [
        rest[offsets[c] - sizes[0]:offsets[c] - sizes[0] + sizes[c]] for c in range(1, CHUNKS)]

    odd = list(range(1, count, 2))
    even = list(range(0, count, 2))
    z_down = [(s, s - 2) for s in range(2, count)]
    swap = [(s, s - 1) for s in odd] + [(s, s + 1) for s in even if s + 1 < count]
    one_down = [(s, s - 1) for s in range(1, count)]
    even_snp = lax.axis_index("snp") % 2 == 0

    even_me = me % 2 == 0
    low = me < 2
    partner = [(j, j ^ 1) for j in range(groups)]
    across = [(j, j ^ 2) for j in range(groups)]

    names = ("two", "swapped", "one", "three", "tiles", "first", "results")
    state = {name: [None] * (CHUNKS + 1) for name in names}

    def finish(c):
        blocks = jnp.concatenate([
            pieces[c],
            state["one"][c],
            state["two"][c],
            state["three"][c],
        ], axis=0)
        gram = jnp.einsum("ab,cb->ac", own_block, blocks, preferred_element_type=jnp.float32)
        size = sizes[c]
        tiles = [gram[:, k * size:(k + 1) * size] for k in range(BAND + 1)]
        state["tiles"][c] = tiles
        payload = jnp.where(even_me, jnp.concatenate([tiles[1], tiles[3]], axis=1),
                            jnp.concatenate([tiles[0], tiles[2]], axis=1))
        state["first"][c] = lax.ppermute(payload, "samp", partner)
        if c >= CHUNKS - 2:
            second_level(c)

    def pick(c, a, b, d, e):
        t = state["tiles"][c]
        return jnp.where(low, jnp.where(even_me, t[a], t[b]), jnp.where(even_me, t[d], t[e]))

    def second_level(c):
        got = state["first"][c]
        size = sizes[c]
        mine = jnp.where(low, got[:, :size], got[:, size:])
        onward = jnp.where(low, got[:, size:], got[:, :size])
        last = lax.ppermute(pick(c, 2, 3, 0, 1) + onward, "samp", across)
        state["results"][c] = pick(c, 0, 1, 2, 3) + mine + last

    ready = [c + 3 for c in range(CHUNKS - 1)] + [CHUNKS + 1]
    for t in range(CHUNKS + 2):
        new = t if t < CHUNKS else None
        second = t - 1 if 0 <= t - 1 < CHUNKS else None
        third = t - 2 if 0 <= t - 2 < CHUNKS - 1 else None
        if new is not None or third is not None:
            sent = moved(joined([pieces[new] if new is not None else None,
                                 state["one"][third] if third is not None else None]), z_down)
            if new is not None:
                state["two"][new] = sent[:sizes[new]]
            if third is not None:
                state["three"][third] = sent[-sizes[third]:]
        if new is not None or second is not None:
            if new is not None and second is not None:
                height = max(sizes[new], sizes[second])
                padded = [jnp.pad(x, ((0, height - x.shape[0]), (0, 0))) for x in (state["two"][second], pieces[new])]
                payload = jnp.where(even_snp, padded[0], padded[1])
            else:
                payload = pieces[new] if new is not None else state["two"][second]
            state["swapped"][t] = moved(payload, swap)
        if second is not None:
            size = sizes[second]
            state["one"][second] = jnp.where(even_snp, state["swapped"][second][:size], state["swapped"][t][:size])
        if second == CHUNKS - 1:
            state["three"][second] = moved(state["two"][second], one_down)
        for c in [c for c in range(CHUNKS) if ready[c] == t]:
            finish(c)
        if 0 <= t - 4 < CHUNKS - 2:
            second_level(t - 4)
        flat, tree = jax.tree.flatten(state)
        following = pieces[t + 1] if t + 1 < CHUNKS else own_block[:8]
        flat, following = lax.optimization_barrier((flat, following))
        state = {k: list(v) for k, v in jax.tree.unflatten(tree, flat).items()}
        if t + 1 < CHUNKS:
            pieces[t + 1] = following
    summed = jnp.concatenate(state["results"][:CHUNKS], axis=1)
    return summed / total


def solution(mesh):
    return jax.shard_map(
        local,
        mesh=mesh,
        in_specs=(P("snp", "samp"),),
        out_specs=P("snp", "samp"),
        check_vma=False,
    )
```

```python
import jax
import jax.numpy as jnp
from jax import lax
from jax.sharding import PartitionSpec as P

BAND = 3
CHUNKS = 8


def moved(value, pairs):
    return lax.ppermute(value, "snp", pairs)


def standardize(values, sums, squares, total):
    mean = sums / total
    variance = squares / total - mean * mean
    return ((values - mean[:, None]) * lax.rsqrt(variance + 1e-05)[:, None]).astype(jnp.bfloat16)


def local_moments(values):
    return (jnp.sum(values, axis=1), jnp.sum(values * values, axis=1))


def joined(parts):
    parts = [p for p in parts if p is not None]
    return parts[0] if len(parts) == 1 else jnp.concatenate(parts, axis=0)


def local(dosages):
    total = dosages.shape[1] * lax.axis_size("samp")
    count = lax.axis_size("snp")
    groups = lax.axis_size("samp")
    me = lax.axis_index("samp")
    flips = list(range(1, groups))

    def choose(values):
        ordered = []
        for k in range(groups):
            pick = values[0]
            for i in flips:
                pick = jnp.where(jnp.bitwise_xor(me, i) == k, values[i], pick)
            ordered.append(pick)
        return ordered

    def added(values):
        ordered = choose(values)
        result = ordered[0]
        for part in ordered[1:]:
            result = result + part
        return result

    def standard_rows(values):
        moments = jnp.stack(local_moments(values))
        summed = added(
            [moments] + [lax.ppermute(moments, "samp", [(j, j ^ i) for j in range(groups)]) for i in flips])
        return standardize(values, summed[0], summed[1], total)

    rows = dosages.shape[0]
    step = rows // CHUNKS
    sizes = [step + 16] + [step] * (CHUNKS - 2) + [step - 16]
    offsets = [sum(sizes[:c]) for c in range(CHUNKS)]
    first_piece = standard_rows(dosages[:sizes[0]])
    rest = standard_rows(dosages[sizes[0]:])
    own_block = jnp.concatenate([first_piece, rest], axis=0)
    pieces = [first_piece] + [
        rest[offsets[c] - sizes[0]:offsets[c] - sizes[0] + sizes[c]] for c in range(1, CHUNKS)]

    odd = list(range(1, count, 2))
    even = list(range(0, count, 2))
    z_down = [(s, s - 2) for s in range(2, count)]
    swap = [(s, s - 1) for s in odd] + [(s, s + 1) for s in even if s + 1 < count]
    one_down = [(s, s - 1) for s in range(1, count)]
    even_snp = lax.axis_index("snp") % 2 == 0

    even_me = me % 2 == 0
    low = me < 2
    partner = [(j, j ^ 1) for j in range(groups)]
    across = [(j, j ^ 2) for j in range(groups)]

    names = ("two", "swapped", "one", "three", "tiles", "first", "results")
    state = {name: [None] * (CHUNKS + 1) for name in names}

    def finish(c):
        blocks = jnp.concatenate([
            pieces[c],
            state["one"][c],
            state["two"][c],
            state["three"][c],
        ], axis=0)
        gram = jnp.einsum("ab,cb->ac", own_block, blocks, preferred_element_type=jnp.float32)
        size = sizes[c]
        tiles = [gram[:, k * size:(k + 1) * size] for k in range(BAND + 1)]
        state["tiles"][c] = tiles
        payload = jnp.where(even_me, jnp.concatenate([tiles[1], tiles[3]], axis=1),
                            jnp.concatenate([tiles[0], tiles[2]], axis=1))
        state["first"][c] = lax.ppermute(payload, "samp", partner)
        if c >= CHUNKS - 3:
            second_level(c)

    def pick(c, a, b, d, e):
        t = state["tiles"][c]
        return jnp.where(low, jnp.where(even_me, t[a], t[b]), jnp.where(even_me, t[d], t[e]))

    def second_level(c):
        got = state["first"][c]
        size = sizes[c]
        mine = jnp.where(low, got[:, :size], got[:, size:])
        onward = jnp.where(low, got[:, size:], got[:, :size])
        last = lax.ppermute(pick(c, 2, 3, 0, 1) + onward, "samp", across)
        state["results"][c] = pick(c, 0, 1, 2, 3) + mine + last

    ready = [c + 3 for c in range(CHUNKS - 1)] + [CHUNKS + 1]
    for t in range(CHUNKS + 2):
        new = t if t < CHUNKS else None
        second = t - 1 if 0 <= t - 1 < CHUNKS else None
        third = t - 2 if 0 <= t - 2 < CHUNKS - 1 else None
        if new is not None or third is not None:
            sent = moved(joined([pieces[new] if new is not None else None,
                                 state["one"][third] if third is not None else None]), z_down)
            if new is not None:
                state["two"][new] = sent[:sizes[new]]
            if third is not None:
                state["three"][third] = sent[-sizes[third]:]
        if new is not None or second is not None:
            if new is not None and second is not None:
                height = max(sizes[new], sizes[second])
                padded = [jnp.pad(x, ((0, height - x.shape[0]), (0, 0))) for x in (state["two"][second], pieces[new])]
                payload = jnp.where(even_snp, padded[0], padded[1])
            else:
                payload = pieces[new] if new is not None else state["two"][second]
            state["swapped"][t] = moved(payload, swap)
        if second is not None:
            size = sizes[second]
            state["one"][second] = jnp.where(even_snp, state["swapped"][second][:size], state["swapped"][t][:size])
        if second == CHUNKS - 1:
            state["three"][second] = moved(state["two"][second], one_down)
        for c in [c for c in range(CHUNKS) if ready[c] == t]:
            finish(c)
        if 0 <= t - 4 < CHUNKS - 3:
            second_level(t - 4)
        flat, tree = jax.tree.flatten(state)
        following = pieces[t + 1] if t + 1 < CHUNKS else own_block[:8]
        flat, following = lax.optimization_barrier((flat, following))
        state = {k: list(v) for k, v in jax.tree.unflatten(tree, flat).items()}
        if t + 1 < CHUNKS:
            pieces[t + 1] = following
    summed = jnp.concatenate(state["results"][:CHUNKS], axis=1)
    return summed / total


def solution(mesh):
    return jax.shard_map(
        local,
        mesh=mesh,
        in_specs=(P("snp", "samp"),),
        out_specs=P("snp", "samp"),
        check_vma=False,
    )
```

```python
import jax
import jax.numpy as jnp
from jax import lax
from jax.sharding import PartitionSpec as P

BAND = 3
CHUNKS = 8


def moved(value, pairs):
    return lax.ppermute(value, "snp", pairs)


def standardize(values, sums, squares, total):
    mean = sums / total
    variance = squares / total - mean * mean
    return ((values - mean[:, None]) * lax.rsqrt(variance + 1e-05)[:, None]).astype(jnp.bfloat16)


def local_moments(values):
    return (jnp.sum(values, axis=1), jnp.sum(values * values, axis=1))


def joined(parts):
    parts = [p for p in parts if p is not None]
    return parts[0] if len(parts) == 1 else jnp.concatenate(parts, axis=0)


def local(dosages):
    total = dosages.shape[1] * lax.axis_size("samp")
    count = lax.axis_size("snp")
    groups = lax.axis_size("samp")
    me = lax.axis_index("samp")
    flips = list(range(1, groups))

    def choose(values):
        ordered = []
        for k in range(groups):
            pick = values[0]
            for i in flips:
                pick = jnp.where(jnp.bitwise_xor(me, i) == k, values[i], pick)
            ordered.append(pick)
        return ordered

    def added(values):
        ordered = choose(values)
        result = ordered[0]
        for part in ordered[1:]:
            result = result + part
        return result

    def standard_rows(values):
        moments = jnp.stack(local_moments(values))
        summed = added(
            [moments] + [lax.ppermute(moments, "samp", [(j, j ^ i) for j in range(groups)]) for i in flips])
        return standardize(values, summed[0], summed[1], total)

    rows = dosages.shape[0]
    step = rows // CHUNKS
    sizes = [step + 16] + [step] * (CHUNKS - 2) + [step - 16]
    offsets = [sum(sizes[:c]) for c in range(CHUNKS)]
    first_piece = standard_rows(dosages[:sizes[0]])
    rest = standard_rows(dosages[sizes[0]:])
    own_block = jnp.concatenate([first_piece, rest], axis=0)
    pieces = [first_piece] + [
        rest[offsets[c] - sizes[0]:offsets[c] - sizes[0] + sizes[c]] for c in range(1, CHUNKS)]

    odd = list(range(1, count, 2))
    even = list(range(0, count, 2))
    z_down = [(s, s - 2) for s in range(2, count)]
    swap = [(s, s - 1) for s in odd] + [(s, s + 1) for s in even if s + 1 < count]
    one_down = [(s, s - 1) for s in range(1, count)]
    even_snp = lax.axis_index("snp") % 2 == 0

    even_me = me % 2 == 0
    low = me < 2
    partner = [(j, j ^ 1) for j in range(groups)]
    across = [(j, j ^ 2) for j in range(groups)]

    names = ("two", "swapped", "one", "three", "tiles", "first", "results")
    state = {name: [None] * (CHUNKS + 1) for name in names}

    def finish(c):
        blocks = jnp.concatenate([
            pieces[c],
            state["one"][c],
            state["two"][c],
            state["three"][c],
        ], axis=0)
        gram = jnp.einsum("ab,cb->ac", own_block, blocks, preferred_element_type=jnp.float32)
        size = sizes[c]
        tiles = [gram[:, k * size:(k + 1) * size] for k in range(BAND + 1)]
        state["tiles"][c] = tiles
        payload = jnp.where(even_me, jnp.concatenate([tiles[1], tiles[3]], axis=1),
                            jnp.concatenate([tiles[0], tiles[2]], axis=1))
        state["first"][c] = lax.ppermute(payload, "samp", partner)
        if c >= CHUNKS - 4:
            second_level(c)

    def pick(c, a, b, d, e):
        t = state["tiles"][c]
        return jnp.where(low, jnp.where(even_me, t[a], t[b]), jnp.where(even_me, t[d], t[e]))

    def second_level(c):
        got = state["first"][c]
        size = sizes[c]
        mine = jnp.where(low, got[:, :size], got[:, size:])
        onward = jnp.where(low, got[:, size:], got[:, :size])
        last = lax.ppermute(pick(c, 2, 3, 0, 1) + onward, "samp", across)
        state["results"][c] = pick(c, 0, 1, 2, 3) + mine + last

    ready = [c + 3 for c in range(CHUNKS - 1)] + [CHUNKS + 1]
    for t in range(CHUNKS + 2):
        new = t if t < CHUNKS else None
        second = t - 1 if 0 <= t - 1 < CHUNKS else None
        third = t - 2 if 0 <= t - 2 < CHUNKS - 1 else None
        if new is not None or third is not None:
            sent = moved(joined([pieces[new] if new is not None else None,
                                 state["one"][third] if third is not None else None]), z_down)
            if new is not None:
                state["two"][new] = sent[:sizes[new]]
            if third is not None:
                state["three"][third] = sent[-sizes[third]:]
        if new is not None or second is not None:
            if new is not None and second is not None:
                height = max(sizes[new], sizes[second])
                padded = [jnp.pad(x, ((0, height - x.shape[0]), (0, 0))) for x in (state["two"][second], pieces[new])]
                payload = jnp.where(even_snp, padded[0], padded[1])
            else:
                payload = pieces[new] if new is not None else state["two"][second]
            state["swapped"][t] = moved(payload, swap)
        if second is not None:
            size = sizes[second]
            state["one"][second] = jnp.where(even_snp, state["swapped"][second][:size], state["swapped"][t][:size])
        if second == CHUNKS - 1:
            state["three"][second] = moved(state["two"][second], one_down)
        for c in [c for c in range(CHUNKS) if ready[c] == t]:
            finish(c)
        if 0 <= t - 4 < CHUNKS - 4:
            second_level(t - 4)
        flat, tree = jax.tree.flatten(state)
        following = pieces[t + 1] if t + 1 < CHUNKS else own_block[:8]
        flat, following = lax.optimization_barrier((flat, following))
        state = {k: list(v) for k, v in jax.tree.unflatten(tree, flat).items()}
        if t + 1 < CHUNKS:
            pieces[t + 1] = following
    summed = jnp.concatenate(state["results"][:CHUNKS], axis=1)
    return summed / total


def solution(mesh):
    return jax.shard_map(
        local,
        mesh=mesh,
        in_specs=(P("snp", "samp"),),
        out_specs=P("snp", "samp"),
        check_vma=False,
    )
```

```python
import jax
import jax.numpy as jnp
from jax import lax
from jax.sharding import PartitionSpec as P

BAND = 3
CHUNKS = 8


def moved(value, pairs):
    return lax.ppermute(value, "snp", pairs)


def standardize(values, sums, squares, total):
    mean = sums / total
    variance = squares / total - mean * mean
    return ((values - mean[:, None]) * lax.rsqrt(variance + 1e-05)[:, None]).astype(jnp.bfloat16)


def local_moments(values):
    return (jnp.sum(values, axis=1), jnp.sum(values * values, axis=1))


def joined(parts):
    parts = [p for p in parts if p is not None]
    return parts[0] if len(parts) == 1 else jnp.concatenate(parts, axis=0)


def local(dosages):
    total = dosages.shape[1] * lax.axis_size("samp")
    count = lax.axis_size("snp")
    groups = lax.axis_size("samp")
    me = lax.axis_index("samp")
    flips = list(range(1, groups))

    def choose(values):
        ordered = []
        for k in range(groups):
            pick = values[0]
            for i in flips:
                pick = jnp.where(jnp.bitwise_xor(me, i) == k, values[i], pick)
            ordered.append(pick)
        return ordered

    def added(values):
        ordered = choose(values)
        result = ordered[0]
        for part in ordered[1:]:
            result = result + part
        return result

    def standard_rows(values):
        moments = jnp.stack(local_moments(values))
        summed = added(
            [moments] + [lax.ppermute(moments, "samp", [(j, j ^ i) for j in range(groups)]) for i in flips])
        return standardize(values, summed[0], summed[1], total)

    rows = dosages.shape[0]
    step = rows // CHUNKS
    sizes = [step + 16] + [step] * (CHUNKS - 2) + [step - 16]
    offsets = [sum(sizes[:c]) for c in range(CHUNKS)]
    first_piece = standard_rows(dosages[:sizes[0]])
    rest = standard_rows(dosages[sizes[0]:])
    own_block = jnp.concatenate([first_piece, rest], axis=0)
    pieces = [first_piece] + [
        rest[offsets[c] - sizes[0]:offsets[c] - sizes[0] + sizes[c]] for c in range(1, CHUNKS)]

    odd = list(range(1, count, 2))
    even = list(range(0, count, 2))
    z_down = [(s, s - 2) for s in range(2, count)]
    swap = [(s, s - 1) for s in odd] + [(s, s + 1) for s in even if s + 1 < count]
    one_down = [(s, s - 1) for s in range(1, count)]
    even_snp = lax.axis_index("snp") % 2 == 0

    even_me = me % 2 == 0
    low = me < 2
    partner = [(j, j ^ 1) for j in range(groups)]
    across = [(j, j ^ 2) for j in range(groups)]

    names = ("two", "swapped", "one", "three", "tiles", "first", "results")
    state = {name: [None] * (CHUNKS + 1) for name in names}

    def finish(c):
        blocks = jnp.concatenate([
            pieces[c],
            state["one"][c],
            state["two"][c],
            state["three"][c],
        ], axis=0)
        gram = jnp.einsum("ab,cb->ac", own_block, blocks, preferred_element_type=jnp.float32)
        size = sizes[c]
        tiles = [gram[:, k * size:(k + 1) * size] for k in range(BAND + 1)]
        state["tiles"][c] = tiles
        payload = jnp.where(even_me, jnp.concatenate([tiles[1], tiles[3]], axis=1),
                            jnp.concatenate([tiles[0], tiles[2]], axis=1))
        state["first"][c] = lax.ppermute(payload, "samp", partner)
        if c >= CHUNKS - 3:
            second_level(c)

    def pick(c, a, b, d, e):
        t = state["tiles"][c]
        return jnp.where(low, jnp.where(even_me, t[a], t[b]), jnp.where(even_me, t[d], t[e]))

    def second_level(c):
        got = state["first"][c]
        size = sizes[c]
        mine = jnp.where(low, got[:, :size], got[:, size:])
        onward = jnp.where(low, got[:, size:], got[:, :size])
        last = lax.ppermute(pick(c, 2, 3, 0, 1) + onward, "samp", across)
        state["results"][c] = (pick(c, 0, 1, 2, 3) + mine + last) / total

    ready = [c + 3 for c in range(CHUNKS - 1)] + [CHUNKS + 1]
    for t in range(CHUNKS + 2):
        new = t if t < CHUNKS else None
        second = t - 1 if 0 <= t - 1 < CHUNKS else None
        third = t - 2 if 0 <= t - 2 < CHUNKS - 1 else None
        if new is not None or third is not None:
            sent = moved(joined([pieces[new] if new is not None else None,
                                 state["one"][third] if third is not None else None]), z_down)
            if new is not None:
                state["two"][new] = sent[:sizes[new]]
            if third is not None:
                state["three"][third] = sent[-sizes[third]:]
        if new is not None or second is not None:
            if new is not None and second is not None:
                height = max(sizes[new], sizes[second])
                padded = [jnp.pad(x, ((0, height - x.shape[0]), (0, 0))) for x in (state["two"][second], pieces[new])]
                payload = jnp.where(even_snp, padded[0], padded[1])
            else:
                payload = pieces[new] if new is not None else state["two"][second]
            state["swapped"][t] = moved(payload, swap)
        if second is not None:
            size = sizes[second]
            state["one"][second] = jnp.where(even_snp, state["swapped"][second][:size], state["swapped"][t][:size])
        if second == CHUNKS - 1:
            state["three"][second] = moved(state["two"][second], one_down)
        for c in [c for c in range(CHUNKS) if ready[c] == t]:
            finish(c)
        if 0 <= t - 4 < CHUNKS - 3:
            second_level(t - 4)
        flat, tree = jax.tree.flatten(state)
        following = pieces[t + 1] if t + 1 < CHUNKS else own_block[:8]
        flat, following = lax.optimization_barrier((flat, following))
        state = {k: list(v) for k, v in jax.tree.unflatten(tree, flat).items()}
        if t + 1 < CHUNKS:
            pieces[t + 1] = following
    return jnp.concatenate(state["results"][:CHUNKS], axis=1)


def solution(mesh):
    return jax.shard_map(
        local,
        mesh=mesh,
        in_specs=(P("snp", "samp"),),
        out_specs=P("snp", "samp"),
        check_vma=False,
    )
```

```python
import jax
import jax.numpy as jnp
from jax import lax
from jax.sharding import PartitionSpec as P

BAND = 3
CHUNKS = 8


def moved(value, pairs):
    return lax.ppermute(value, "snp", pairs)


def standardize(values, sums, squares, total):
    mean = sums / total
    variance = squares / total - mean * mean
    return ((values - mean[:, None]) * lax.rsqrt(variance + 1e-05)[:, None]).astype(jnp.bfloat16)


def local_moments(values):
    return (jnp.sum(values, axis=1), jnp.sum(values * values, axis=1))


def joined(parts):
    parts = [p for p in parts if p is not None]
    return parts[0] if len(parts) == 1 else jnp.concatenate(parts, axis=0)


def local(dosages):
    total = dosages.shape[1] * lax.axis_size("samp")
    count = lax.axis_size("snp")
    groups = lax.axis_size("samp")
    me = lax.axis_index("samp")
    flips = list(range(1, groups))

    def choose(values):
        ordered = []
        for k in range(groups):
            pick = values[0]
            for i in flips:
                pick = jnp.where(jnp.bitwise_xor(me, i) == k, values[i], pick)
            ordered.append(pick)
        return ordered

    def added(values):
        ordered = choose(values)
        result = ordered[0]
        for part in ordered[1:]:
            result = result + part
        return result

    def standard_rows(values):
        moments = jnp.stack(local_moments(values))
        summed = added(
            [moments] + [lax.ppermute(moments, "samp", [(j, j ^ i) for j in range(groups)]) for i in flips])
        return standardize(values, summed[0], summed[1], total)

    rows = dosages.shape[0]
    step = rows // CHUNKS
    sizes = [step + 16] + [step] * (CHUNKS - 2) + [step - 16]
    offsets = [sum(sizes[:c]) for c in range(CHUNKS)]
    first_piece = standard_rows(dosages[:sizes[0]])
    rest = standard_rows(dosages[sizes[0]:])
    own_block = jnp.concatenate([first_piece, rest], axis=0)
    pieces = [first_piece] + [
        rest[offsets[c] - sizes[0]:offsets[c] - sizes[0] + sizes[c]] for c in range(1, CHUNKS)]

    odd = list(range(1, count, 2))
    even = list(range(0, count, 2))
    z_down = [(s, s - 2) for s in range(2, count)]
    swap = [(s, s - 1) for s in odd] + [(s, s + 1) for s in even if s + 1 < count]
    one_down = [(s, s - 1) for s in range(1, count)]
    even_snp = lax.axis_index("snp") % 2 == 0

    even_me = me % 2 == 0
    low = me < 2
    partner = [(j, j ^ 1) for j in range(groups)]
    across = [(j, j ^ 2) for j in range(groups)]

    names = ("two", "swapped", "one", "three", "tiles", "first", "results")
    state = {name: [None] * (CHUNKS + 1) for name in names}

    def finish(c):
        blocks = jnp.concatenate([
            pieces[c],
            state["one"][c],
            state["two"][c],
            state["three"][c],
        ], axis=0)
        gram = jnp.einsum("ab,cb->ac", own_block, blocks, preferred_element_type=jnp.float32)
        size = sizes[c]
        tiles = [gram[:, k * size:(k + 1) * size] for k in range(BAND + 1)]
        state["tiles"][c] = tiles
        payload = jnp.where(even_me, jnp.concatenate([tiles[1], tiles[3]], axis=1),
                            jnp.concatenate([tiles[0], tiles[2]], axis=1))
        state["first"][c] = lax.ppermute(payload, "samp", partner)
        if c >= CHUNKS - 2:
            second_level(c)

    def pick(c, a, b, d, e):
        t = state["tiles"][c]
        return jnp.where(low, jnp.where(even_me, t[a], t[b]), jnp.where(even_me, t[d], t[e]))

    def second_level(c):
        got = state["first"][c]
        size = sizes[c]
        mine = jnp.where(low, got[:, :size], got[:, size:])
        onward = jnp.where(low, got[:, size:], got[:, :size])
        last = lax.ppermute(pick(c, 2, 3, 0, 1) + onward, "samp", across)
        state["results"][c] = (pick(c, 0, 1, 2, 3) + mine + last) / total

    ready = [c + 3 for c in range(CHUNKS - 2)] + [CHUNKS, CHUNKS + 1]
    for t in range(CHUNKS + 2):
        new = t if t < CHUNKS else None
        second = t - 1 if 0 <= t - 1 < CHUNKS else None
        third = t - 2 if 0 <= t - 2 < CHUNKS - 2 else None
        if new is not None or third is not None:
            sent = moved(joined([pieces[new] if new is not None else None,
                                 state["one"][third] if third is not None else None]), z_down)
            if new is not None:
                state["two"][new] = sent[:sizes[new]]
            if third is not None:
                state["three"][third] = sent[-sizes[third]:]
        if new is not None or second is not None:
            if new is not None and second is not None:
                height = max(sizes[new], sizes[second])
                padded = [jnp.pad(x, ((0, height - x.shape[0]), (0, 0))) for x in (state["two"][second], pieces[new])]
                payload = jnp.where(even_snp, padded[0], padded[1])
            else:
                payload = pieces[new] if new is not None else state["two"][second]
            state["swapped"][t] = moved(payload, swap)
        if second is not None:
            size = sizes[second]
            state["one"][second] = jnp.where(even_snp, state["swapped"][second][:size], state["swapped"][t][:size])
        if second is not None and second >= CHUNKS - 2:
            state["three"][second] = moved(state["two"][second], one_down)
        for c in [c for c in range(CHUNKS) if ready[c] == t]:
            finish(c)
        if 0 <= t - 4 < CHUNKS - 2:
            second_level(t - 4)
        flat, tree = jax.tree.flatten(state)
        following = pieces[t + 1] if t + 1 < CHUNKS else own_block[:8]
        flat, following = lax.optimization_barrier((flat, following))
        state = {k: list(v) for k, v in jax.tree.unflatten(tree, flat).items()}
        if t + 1 < CHUNKS:
            pieces[t + 1] = following
    return jnp.concatenate(state["results"][:CHUNKS], axis=1)


def solution(mesh):
    return jax.shard_map(
        local,
        mesh=mesh,
        in_specs=(P("snp", "samp"),),
        out_specs=P("snp", "samp"),
        check_vma=False,
    )
```
